32 devices in a mesh: node: 4 (over x, core), dev: 8 (over z, y).
Axes of the slice: x: 2, y: 2, z: 4, core: 2. Of those that a mesh axis runs over, the one named last changes fastest.
Arguments:
- state: float32 [2, 524288], P(None, ('node', 'dev')), may hold values from -6 to 6
- gates: float32 [4, 2, 128, 128], replicated, may hold values from -0.375 to 0.375
- qubit_order: int32 [14], replicated, may hold values from 0 to 13, each once
Outputs:
- final_state: float32 [2, 524288], P(None, ('node', 'dev'))
The draws below stay inside these ranges and needn't reach their ends.
Inputs may be any that keep to these rules, and one draw needn't show every extreme that they name: `qubit_order`: a permutation of 0 to 13.
All inputs are finite; a program needn't handle non-finite values.
Results may differ from the reference program's by a relative error of at most 0.00007.
Values sent between devices are 32-bit elements; how exact they have to be, the bound alone decides.
No kernel may reach another device: no remote copies, remote signals or barrier semaphores. Data moves between devices by JAX's collectives and lax.ppermute only.
A program may use at most 64 MiB of HBM per device.

```python
import jax
import jax.numpy as jnp
from jax import lax

AMP_DEV = 16384
GQ = 7
NGATES = 4
GATE = 128
AMPS = 524288
N_NODE = 4
N_DEV = 8


def steps_of(own_key, extent, shards, smallest, top_value):
    factor_of, own = 1.0, jax.random.fold_in(own_key, 6)
    for axis_at, shards_of in shards:
        steps = jnp.exp(jax.random.uniform(jax.random.fold_in(own, axis_at), (shards_of,), jnp.float32, smallest / len(shards), top_value / len(shards)))
        factor_of = factor_of * jnp.repeat(steps, extent[axis_at] // shards_of).reshape([-1 if axis == axis_at else 1 for axis in range(len(extent))])
    return factor_of


def scatter_about(own_key, dims, spread, reach, shards=(), held_as=jnp.bfloat16):
    result = spread * jax.random.normal(own_key, dims, jnp.float32)
    if shards:
        result = result * steps_of(own_key, dims, shards, -0.22, 0.18)
    return jnp.clip(result, -reach, reach).astype(held_as)


def setup_inputs(seed: int = 0) -> dict:
    streams_of = jax.random.split(jax.random.key(seed), 4)
    state = scatter_about(streams_of[0], (2, AMPS), 1.0, 6.0, ((1, 32),), jnp.float32)
    gates = scatter_about(streams_of[1], (NGATES, 2, GATE, GATE), (2 * GATE) ** -0.5, 0.375, (), jnp.float32)
    qubit_order = jax.random.permutation(streams_of[2], 2 * GQ).astype(jnp.int32)
    return dict(state=state, gates=gates, qubit_order=qubit_order)


def order_low(planes, qubit_order, gbits):
    low = 2 ** (2 * gbits)
    positions = lax.iota(jnp.int32, low)
    source = jnp.zeros((low,), jnp.int32)
    for j in range(2 * gbits):
        source = source + jnp.left_shift(jnp.right_shift(positions, j) & 1, qubit_order[j].astype(jnp.int32))
    blocks = planes.reshape(2, -1, low)
    return jnp.take(blocks, source, axis=2).reshape(2, -1)


def apply_gate(planes, gate, start, gbits):
    width = 2 ** gbits
    total = planes.shape[1]
    lower = 2 ** start
    upper = total // (lower * width)
    real_part = planes[0].reshape(upper, width, lower)
    imag_part = planes[1].reshape(upper, width, lower)

    def product(matrix, vector):
        return jnp.einsum("rc,hco->hro", matrix, vector, precision=lax.Precision.HIGHEST)

    new_real = product(gate[0], real_part) - product(gate[1], imag_part)
    new_imag = product(gate[0], imag_part) + product(gate[1], real_part)
    return jnp.stack([new_real.reshape(-1), new_imag.reshape(-1)])


def reference(state, gates, qubit_order):
    gbits = GQ
    lbits = AMP_DEV.bit_length() - 1
    planes = order_low(state, qubit_order, gbits)
    planes = apply_gate(planes, gates[0], 0, gbits)
    planes = apply_gate(planes, gates[1], gbits, gbits)
    rest = AMP_DEV // (N_NODE * N_DEV)
    view = planes.reshape(2, N_NODE, N_DEV, N_DEV, N_NODE, rest)
    planes = jnp.transpose(view, (0, 4, 3, 2, 1, 5)).reshape(2, -1)
    planes = apply_gate(planes, gates[2], lbits - gbits, gbits)
    planes = apply_gate(planes, gates[3], gbits, gbits)
    return planes
```

```python
import jax
import jax.numpy as jnp
from jax import lax
from jax.sharding import PartitionSpec as P

HI = lax.Precision.HIGHEST


def mm(a, b):
    return jnp.matmul(a, b, precision=HI)


def layout_maps(qubit_order, gbits):
    width = 2**gbits
    q = qubit_order.astype(jnp.int32)
    j = jnp.arange(2 * gbits)
    crossing = jnp.where(j < gbits, q >= gbits, q < gbits).reshape(2, gbits)
    k = jnp.sum(crossing[0].astype(jnp.int32))
    cross_i = crossing.astype(jnp.int32)
    before_cross = jnp.cumsum(cross_i, axis=1) - cross_i
    before_stay = jnp.cumsum(1 - cross_i, axis=1) - (1 - cross_i)
    pos = jnp.where(crossing, before_cross, k + before_stay).reshape(2 * gbits)
    iota = jnp.arange(width, dtype=jnp.int32)
    bits = jnp.right_shift(iota[None, :], (q % gbits)[:, None]) & 1
    contrib = jnp.left_shift(bits, pos[:, None])
    row_to = jnp.sum(jnp.where(q[:, None] >= gbits, contrib, 0), axis=0)
    col_to = jnp.sum(jnp.where(q[:, None] < gbits, contrib, 0), axis=0)
    own = jnp.right_shift(iota[None, :], jnp.arange(gbits)[:, None]) & 1
    row_from = jnp.sum(jnp.left_shift(own, pos[gbits:, None]), axis=0)
    col_from = jnp.sum(jnp.left_shift(own, pos[:gbits, None]), axis=0)
    f32 = jnp.float32
    a = (iota[:, None] == row_to[None, :]).astype(f32)
    b = (col_to[:, None] == iota[None, :]).astype(f32)
    c = (row_from[:, None] == iota[None, :]).astype(f32)
    d = (iota[:, None] == col_from[None, :]).astype(f32)
    return a, b, c, d, k


def swap_low_bits(planes, k, gbits):
    width = 2**gbits
    rows = lax.broadcasted_iota(jnp.int32, (width, width), 0)
    cols = lax.broadcasted_iota(jnp.int32, (width, width), 1)
    for u in range(gbits):
        hi = 2 ** (gbits - 1 - u)
        lo = 2**u
        view = planes.reshape(2, hi, 2, lo, hi, 2, lo)
        flipped = jnp.flip(view, axis=(2, 5)).reshape(planes.shape)
        differ = (jnp.right_shift(rows, u) & 1) != (jnp.right_shift(cols, u) & 1)
        take = differ & (u < k)
        planes = jnp.where(take[None], flipped, planes)
    return planes


def cmul_left(gr, gi, xr, xi):
    return mm(gr, xr) - mm(gi, xi), mm(gr, xi) + mm(gi, xr)


def cmul_right(xr, xi, hr, hi):
    return mm(xr, hr) - mm(xi, hi), mm(xr, hi) + mm(xi, hr)


def local(state, gates, qubit_order):
    gbits = gates.shape[-1].bit_length() - 1
    width = 2**gbits
    amps = state.shape[1]
    a, b, c, d, k = layout_maps(qubit_order, gbits)
    planes = state.reshape(2, width, width)
    planes = jnp.einsum("xr,prc,cy->pxy", a, planes, b, precision=HI)
    planes = swap_low_bits(planes, k, gbits)
    g0 = gates[0]
    g1 = gates[1]
    h0r = mm(d, g0[0].T)
    h0i = mm(d, g0[1].T)
    g1r = mm(g1[0], c)
    g1i = mm(g1[1], c)
    ur, ui = cmul_right(planes[0], planes[1], h0r, h0i)
    yr, yi = cmul_left(g1r, g1i, ur, ui)
    n_dev = lax.axis_size("dev")
    n_node = lax.axis_size("node")
    blocks = jnp.stack([yr, yi]).reshape(2, n_dev * n_node, -1)
    blocks = lax.all_to_all(blocks, ("dev", "node"), 1, 1, tiled=True)
    w = blocks.reshape(2, width, amps // width)
    g2 = gates[2]
    g3 = gates[3]
    vr, vi = cmul_left(g2[0], g2[1], w[0], w[1])
    zr, zi = cmul_left(g3[0], g3[1], vr, vi)
    return jnp.stack([zr.reshape(-1), zi.reshape(-1)])


def solution(mesh):
    return jax.shard_map(
        local,
        mesh=mesh,
        in_specs=(P(None, ("node", "dev")), P(), P()),
        out_specs=P(None, ("node", "dev")),
        check_vma=False,
    )
```

```python
import jax
import jax.numpy as jnp
from jax import lax
from jax.experimental import pallas as pl
from jax.experimental.pallas import tpu as pltpu
from jax.sharding import PartitionSpec as P

HI = lax.Precision.HIGHEST
F32 = jnp.float32


def mm(a, b):
    return jnp.dot(a, b, precision=HI, preferred_element_type=F32)


def mm_t(a, b):
    return lax.dot_general(a, b, (((1,), (1,)), ((), ())), precision=HI, preferred_element_type=F32)


def flip_bit(x, index, u, axis):
    n = x.shape[axis]
    step = 2**u
    one = pltpu.roll(x, step, axis)
    other = pltpu.roll(x, n - step, axis)
    moved = pltpu.roll(index, step, axis)
    return jnp.where(moved == (index ^ step), one, other)


def first_kernel(q_ref, s_ref, g_ref, y_ref, *, gbits):
    width = 2**gbits
    q = [q_ref[j] for j in range(2 * gbits)]
    is_row_src = [jnp.where(q[j] >= gbits, 1, 0) for j in range(2 * gbits)]
    crossing = [is_row_src[j] if j < gbits else 1 - is_row_src[j] for j in range(2 * gbits)]
    k = sum(crossing[:gbits])
    pos = []
    for group in range(2):
        n_cross = 0
        n_stay = 0
        for t in range(gbits):
            cr = crossing[group * gbits + t]
            pos.append(jnp.where(cr == 1, n_cross, k + n_stay))
            n_cross = n_cross + cr
            n_stay = n_stay + (1 - cr)
    rows = lax.broadcasted_iota(jnp.int32, (width, width), 0)
    cols = lax.broadcasted_iota(jnp.int32, (width, width), 1)
    row_to = jnp.zeros((width, width), jnp.int32)
    col_to = jnp.zeros((width, width), jnp.int32)
    for j in range(2 * gbits):
        bit_at = q[j] - gbits * is_row_src[j]
        row_to = row_to + is_row_src[j] * jnp.left_shift(jnp.right_shift(cols, bit_at) & 1, pos[j])
        col_to = col_to + (1 - is_row_src[j]) * jnp.left_shift(jnp.right_shift(rows, bit_at) & 1, pos[j])
    row_from = jnp.zeros((width, width), jnp.int32)
    col_from = jnp.zeros((width, width), jnp.int32)
    for t in range(gbits):
        row_from = row_from + jnp.left_shift(jnp.right_shift(rows, t) & 1, pos[gbits + t])
        col_from = col_from + jnp.left_shift(jnp.right_shift(cols, t) & 1, pos[t])
    a = (rows == row_to).astype(F32)
    b = (cols == col_to).astype(F32)
    c = (cols == row_from).astype(F32)
    d = (rows == col_from).astype(F32)
    planes = []
    for p in range(2):
        x = mm(mm(a, s_ref[p]), b)
        for u in range(gbits):
            flipped = flip_bit(flip_bit(x, rows, u, 0), cols, u, 1)
            differ = (jnp.right_shift(rows ^ cols, u) & 1) == 1
            x = jnp.where(differ & (u < k), flipped, x)
        planes.append(x)
    xr, xi = planes
    h0r = mm_t(d, g_ref[0, 0])
    h0i = mm_t(d, g_ref[0, 1])
    g1r = mm(g_ref[1, 0], c)
    g1i = mm(g_ref[1, 1], c)
    ur = mm(xr, h0r) - mm(xi, h0i)
    ui = mm(xr, h0i) + mm(xi, h0r)
    y_ref[0] = mm(g1r, ur) - mm(g1i, ui)
    y_ref[1] = mm(g1r, ui) + mm(g1i, ur)


def second_kernel(w_ref, g_ref, z_ref):
    wr = w_ref[0]
    wi = w_ref[1]
    vr = mm(g_ref[0, 0], wr) - mm(g_ref[0, 1], wi)
    vi = mm(g_ref[0, 0], wi) + mm(g_ref[0, 1], wr)
    z_ref[0] = mm(g_ref[1, 0], vr) - mm(g_ref[1, 1], vi)
    z_ref[1] = mm(g_ref[1, 0], vi) + mm(g_ref[1, 1], vr)


def local(state, gates, qubit_order):
    gbits = gates.shape[-1].bit_length() - 1
    width = 2**gbits
    planes = state.reshape(2, width, width)
    y = pl.pallas_call(
        lambda *refs: first_kernel(*refs, gbits=gbits),
        out_shape=jax.ShapeDtypeStruct((2, width, width), F32),
        grid=(1,),
        in_specs=[
            pl.BlockSpec(memory_space=pltpu.SMEM),
            pl.BlockSpec((2, width, width), lambda i: (0, 0, 0)),
            pl.BlockSpec((2, 2, width, width), lambda i: (0, 0, 0, 0)),
        ],
        out_specs=pl.BlockSpec((2, width, width), lambda i: (0, 0, 0)),
    )(qubit_order.astype(jnp.int32), planes, gates)
    parts = lax.axis_size("dev") * lax.axis_size("node")
    if width % parts == 0:
        w = lax.all_to_all(y, ("dev", "node"), 1, 1, tiled=True)
    else:
        w = lax.all_to_all(y.reshape(2, parts, -1), ("dev", "node"), 1, 1, tiled=True)
        w = w.reshape(2, width, width)
    z = pl.pallas_call(
        second_kernel,
        out_shape=jax.ShapeDtypeStruct((2, width, width), F32),
        grid=(1,),
        in_specs=[
            pl.BlockSpec((2, width, width), lambda i: (0, 0, 0)),
            pl.BlockSpec((2, 2, width, width), lambda i: (1, 0, 0, 0)),
        ],
        out_specs=pl.BlockSpec((2, width, width), lambda i: (0, 0, 0)),
    )(w, gates)
    return z.reshape(2, -1)


def solution(mesh):
    return jax.shard_map(
        local,
        mesh=mesh,
        in_specs=(P(None, ("node", "dev")), P(), P()),
        out_specs=P(None, ("node", "dev")),
        check_vma=False,
    )
```

```python
import jax
import jax.numpy as jnp
from jax import lax
from jax.experimental import pallas as pl
from jax.experimental.pallas import tpu as pltpu
from jax.sharding import PartitionSpec as P

HI = lax.Precision.HIGHEST
F32 = jnp.float32


def mm(a, b):
    return jnp.dot(a, b, precision=HI, preferred_element_type=F32)


def mm_t(a, b):
    return lax.dot_general(a, b, (((1,), (1,)), ((), ())), precision=HI, preferred_element_type=F32)


def flip_bit(x, index, u, axis):
    n = x.shape[axis]
    step = 2**u
    one = pltpu.roll(x, step, axis)
    other = pltpu.roll(x, n - step, axis)
    moved = pltpu.roll(index, step, axis)
    return jnp.where(moved == (index ^ step), one, other)


def first_kernel(q_ref, s_ref, g_ref, y_ref, *, gbits):
    width = 2**gbits
    q = [q_ref[j] for j in range(2 * gbits)]
    is_row_src = [jnp.where(q[j] >= gbits, 1, 0) for j in range(2 * gbits)]
    crossing = [is_row_src[j] if j < gbits else 1 - is_row_src[j] for j in range(2 * gbits)]
    k = sum(crossing[:gbits])
    pos = []
    for group in range(2):
        n_cross = 0
        n_stay = 0
        for t in range(gbits):
            cr = crossing[group * gbits + t]
            pos.append(jnp.where(cr == 1, n_cross, k + n_stay))
            n_cross = n_cross + cr
            n_stay = n_stay + (1 - cr)
    rows = lax.broadcasted_iota(jnp.int32, (width, width), 0)
    cols = lax.broadcasted_iota(jnp.int32, (width, width), 1)
    row_to = jnp.zeros((width, width), jnp.int32)
    col_to = jnp.zeros((width, width), jnp.int32)
    for j in range(2 * gbits):
        bit_at = q[j] - gbits * is_row_src[j]
        row_to = row_to + is_row_src[j] * jnp.left_shift(jnp.right_shift(cols, bit_at) & 1, pos[j])
        col_to = col_to + (1 - is_row_src[j]) * jnp.left_shift(jnp.right_shift(rows, bit_at) & 1, pos[j])
    row_from = jnp.zeros((width, width), jnp.int32)
    col_from = jnp.zeros((width, width), jnp.int32)
    for t in range(gbits):
        row_from = row_from + jnp.left_shift(jnp.right_shift(rows, t) & 1, pos[gbits + t])
        col_from = col_from + jnp.left_shift(jnp.right_shift(cols, t) & 1, pos[t])
    a = (rows == row_to).astype(F32)
    b = (cols == col_to).astype(F32)
    c = (cols == row_from).astype(F32)
    d = (rows == col_from).astype(F32)
    planes = []
    for p in range(2):
        x = mm(mm(a, s_ref[pl.ds(p, width, stride=2), :]), b)
        for u in range(gbits):
            flipped = flip_bit(flip_bit(x, rows, u, 0), cols, u, 1)
            differ = (jnp.right_shift(rows ^ cols, u) & 1) == 1
            x = jnp.where(differ & (u < k), flipped, x)
        planes.append(x)
    xr, xi = planes
    h0r = mm_t(d, g_ref[0, 0])
    h0i = mm_t(d, g_ref[0, 1])
    g1r = mm(g_ref[1, 0], c)
    g1i = mm(g_ref[1, 1], c)
    ur = mm(xr, h0r) - mm(xi, h0i)
    ui = mm(xr, h0i) + mm(xi, h0r)
    y_ref[pl.ds(0, width, stride=2), :] = mm(g1r, ur) - mm(g1i, ui)
    y_ref[pl.ds(1, width, stride=2), :] = mm(g1r, ui) + mm(g1i, ur)


def second_kernel(w_ref, g_ref, z_ref):
    width = g_ref.shape[-1]
    wr = w_ref[pl.ds(0, width, stride=2), :]
    wi = w_ref[pl.ds(1, width, stride=2), :]
    vr = mm(g_ref[0, 0], wr) - mm(g_ref[0, 1], wi)
    vi = mm(g_ref[0, 0], wi) + mm(g_ref[0, 1], wr)
    z_ref[pl.ds(0, width, stride=2), :] = mm(g_ref[1, 0], vr) - mm(g_ref[1, 1], vi)
    z_ref[pl.ds(1, width, stride=2), :] = mm(g_ref[1, 0], vi) + mm(g_ref[1, 1], vr)


def exchange(y, width):
    parts = lax.axis_size("dev") * lax.axis_size("node")
    axes = ("dev", "node")
    if width % parts == 0:
        return lax.all_to_all(y, axes, 0, 0, tiled=True)
    split = parts // width
    v = y.reshape(width, 2, split, width // split).transpose(0, 2, 1, 3)
    v = lax.all_to_all(v.reshape(parts, -1), axes, 0, 0, tiled=True)
    v = v.reshape(width, split, 2, width // split).transpose(0, 2, 1, 3)
    return v.reshape(width, 2, width)


def local(state, gates, qubit_order):
    gbits = gates.shape[-1].bit_length() - 1
    width = 2**gbits
    rows = state.reshape(2, width, width).transpose(1, 0, 2).reshape(2 * width, width)
    y = pl.pallas_call(
        lambda *refs: first_kernel(*refs, gbits=gbits),
        out_shape=jax.ShapeDtypeStruct((2 * width, width), F32),
        grid=(1,),
        in_specs=[
            pl.BlockSpec(memory_space=pltpu.SMEM),
            pl.BlockSpec((2 * width, width), lambda i: (0, 0)),
            pl.BlockSpec((2, 2, width, width), lambda i: (0, 0, 0, 0)),
        ],
        out_specs=pl.BlockSpec((2 * width, width), lambda i: (0, 0)),
    )(qubit_order.astype(jnp.int32), rows, gates)
    w = exchange(y.reshape(width, 2, width), width).reshape(2 * width, width)
    z = pl.pallas_call(
        second_kernel,
        out_shape=jax.ShapeDtypeStruct((2 * width, width), F32),
        grid=(1,),
        in_specs=[
            pl.BlockSpec((2 * width, width), lambda i: (0, 0)),
            pl.BlockSpec((2, 2, width, width), lambda i: (1, 0, 0, 0)),
        ],
        out_specs=pl.BlockSpec((2 * width, width), lambda i: (0, 0)),
    )(w, gates)
    return z.reshape(width, 2, width).transpose(1, 0, 2).reshape(2, -1)


def solution(mesh):
    return jax.shard_map(
        local,
        mesh=mesh,
        in_specs=(P(None, ("node", "dev")), P(), P()),
        out_specs=P(None, ("node", "dev")),
        check_vma=False,
    )
```

```python
import jax
import jax.numpy as jnp
from jax import lax
from jax.experimental import pallas as pl
from jax.experimental.pallas import tpu as pltpu
from jax.sharding import PartitionSpec as P

HI = lax.Precision.HIGHEST
F32 = jnp.float32


def mm(a, b):
    return jnp.dot(a, b, precision=HI, preferred_element_type=F32)


def mm_t(a, b):
    return lax.dot_general(a, b, (((1,), (1,)), ((), ())), precision=HI, preferred_element_type=F32)


def flip_bit(x, index, u, axis):
    n = x.shape[axis]
    step = 2**u
    one = pltpu.roll(x, step, axis)
    other = pltpu.roll(x, n - step, axis)
    moved = pltpu.roll(index, step, axis)
    return jnp.where(moved == (index ^ step), one, other)


def complex_block(gr, gi):
    return jnp.concatenate(
        [jnp.concatenate([gr, -gi], axis=1), jnp.concatenate([gi, gr], axis=1)], axis=0
    )


def first_kernel(q_ref, s_ref, g_ref, y_ref, *, gbits):
    width = 2**gbits
    q = [q_ref[j] for j in range(2 * gbits)]
    is_row_src = [jnp.where(q[j] >= gbits, 1, 0) for j in range(2 * gbits)]
    crossing = [is_row_src[j] if j < gbits else 1 - is_row_src[j] for j in range(2 * gbits)]
    k = sum(crossing[:gbits])
    pos = []
    for group in range(2):
        n_cross = 0
        n_stay = 0
        for t in range(gbits):
            cr = crossing[group * gbits + t]
            pos.append(jnp.where(cr == 1, n_cross, k + n_stay))
            n_cross = n_cross + cr
            n_stay = n_stay + (1 - cr)
    lane = lax.broadcasted_iota(jnp.int32, (1, width), 1)
    row_to = jnp.zeros((1, width), jnp.int32)
    col_to = jnp.zeros((1, width), jnp.int32)
    for j in range(2 * gbits):
        bit = jnp.left_shift(jnp.right_shift(lane, q[j] - gbits * is_row_src[j]) & 1, pos[j])
        row_to = row_to + is_row_src[j] * bit
        col_to = col_to + (1 - is_row_src[j]) * bit
    row_from = jnp.zeros((1, width), jnp.int32)
    col_from = jnp.zeros((1, width), jnp.int32)
    for t in range(gbits):
        row_from = row_from + jnp.left_shift(jnp.right_shift(lane, t) & 1, pos[gbits + t])
        col_from = col_from + jnp.left_shift(jnp.right_shift(lane, t) & 1, pos[t])
    rows = lax.broadcasted_iota(jnp.int32, (width, width), 0)
    a = (rows == row_to).astype(F32)
    b_t = (rows == col_to).astype(F32)
    c_t = (rows == row_from).astype(F32)
    d = (rows == col_from).astype(F32)
    sr = s_ref[pl.ds(0, width, stride=2), :]
    si = s_ref[pl.ds(1, width, stride=2), :]
    x = mm(a, jnp.concatenate([sr, si], axis=1))
    x = mm_t(jnp.concatenate([x[:, :width], x[:, width:]], axis=0), b_t)
    rows2 = lax.broadcasted_iota(jnp.int32, (2 * width, width), 0)
    cols2 = lax.broadcasted_iota(jnp.int32, (2 * width, width), 1)
    for u in range(gbits):
        flipped = flip_bit(flip_bit(x, rows2, u, 0), cols2, u, 1)
        differ = (jnp.right_shift(rows2 ^ cols2, u) & 1) == 1
        x = jnp.where(differ & (u < k), flipped, x)
    h0 = mm_t(d, jnp.concatenate([g_ref[0, 0], g_ref[0, 1]], axis=0))
    h0r = h0[:, :width]
    h0i = h0[:, width:]
    u_ri = mm(jnp.concatenate([x[:width], x[width:]], axis=1), jnp.concatenate(
        [jnp.concatenate([h0r, h0i], axis=1), jnp.concatenate([-h0i, h0r], axis=1)], axis=0
    ))
    g1 = mm_t(jnp.concatenate([g_ref[1, 0], g_ref[1, 1]], axis=0), c_t)
    y = mm(complex_block(g1[:width], g1[width:]), jnp.concatenate([u_ri[:, :width], u_ri[:, width:]], axis=0))
    y_ref[pl.ds(0, width, stride=2), :] = y[:width]
    y_ref[pl.ds(1, width, stride=2), :] = y[width:]


def second_kernel(w_ref, g_ref, z_ref):
    width = g_ref.shape[-1]
    w = jnp.concatenate([w_ref[pl.ds(0, width, stride=2), :], w_ref[pl.ds(1, width, stride=2), :]], axis=0)
    v = mm(complex_block(g_ref[0, 0], g_ref[0, 1]), w)
    z = mm(complex_block(g_ref[1, 0], g_ref[1, 1]), v)
    z_ref[pl.ds(0, width, stride=2), :] = z[:width]
    z_ref[pl.ds(1, width, stride=2), :] = z[width:]


def exchange(y, width):
    parts = lax.axis_size("dev") * lax.axis_size("node")
    axes = ("dev", "node")
    if width % parts == 0:
        return lax.all_to_all(y, axes, 0, 0, tiled=True)
    split = parts // width
    v = y.reshape(width, 2, split, width // split).transpose(0, 2, 1, 3)
    v = lax.all_to_all(v.reshape(parts, -1), axes, 0, 0, tiled=True)
    v = v.reshape(width, split, 2, width // split).transpose(0, 2, 1, 3)
    return v.reshape(width, 2, width)


def local(state, gates, qubit_order):
    gbits = gates.shape[-1].bit_length() - 1
    width = 2**gbits
    rows = state.reshape(2, width, width).transpose(1, 0, 2).reshape(2 * width, width)
    y = pl.pallas_call(
        lambda *refs: first_kernel(*refs, gbits=gbits),
        out_shape=jax.ShapeDtypeStruct((2 * width, width), F32),
        grid=(1,),
        in_specs=[
            pl.BlockSpec(memory_space=pltpu.SMEM),
            pl.BlockSpec((2 * width, width), lambda i: (0, 0)),
            pl.BlockSpec((2, 2, width, width), lambda i: (0, 0, 0, 0)),
        ],
        out_specs=pl.BlockSpec((2 * width, width), lambda i: (0, 0)),
    )(qubit_order.astype(jnp.int32), rows, gates)
    w = exchange(y.reshape(width, 2, width), width).reshape(2 * width, width)
    z = pl.pallas_call(
        second_kernel,
        out_shape=jax.ShapeDtypeStruct((2 * width, width), F32),
        grid=(1,),
        in_specs=[
            pl.BlockSpec((2 * width, width), lambda i: (0, 0)),
            pl.BlockSpec((2, 2, width, width), lambda i: (1, 0, 0, 0)),
        ],
        out_specs=pl.BlockSpec((2 * width, width), lambda i: (0, 0)),
    )(w, gates)
    return z.reshape(width, 2, width).transpose(1, 0, 2).reshape(2, -1)


def solution(mesh):
    return jax.shard_map(
        local,
        mesh=mesh,
        in_specs=(P(None, ("node", "dev")), P(), P()),
        out_specs=P(None, ("node", "dev")),
        check_vma=False,
    )
```

```python
import jax
import jax.numpy as jnp
from jax import lax
from jax.experimental import pallas as pl
from jax.experimental.pallas import tpu as pltpu
from jax.sharding import PartitionSpec as P

HI = lax.Precision.HIGHEST
F32 = jnp.float32


def mm(a, b):
    return jnp.dot(a, b, precision=HI, preferred_element_type=F32)


def mm_t(a, b):
    return lax.dot_general(a, b, (((1,), (1,)), ((), ())), precision=HI, preferred_element_type=F32)


def flip_bit(x, index, u, axis):
    n = x.shape[axis]
    step = 2**u
    one = pltpu.roll(x, step, axis)
    other = pltpu.roll(x, n - step, axis)
    moved = pltpu.roll(index, step, axis)
    return jnp.where(moved == (index ^ step), one, other)


def complex_block(gr, gi):
    return jnp.concatenate(
        [jnp.concatenate([gr, -gi], axis=1), jnp.concatenate([gi, gr], axis=1)], axis=0
    )


def first_kernel(q_ref, s_ref, g_ref, y_ref, *, gbits):
    width = 2**gbits
    q = [q_ref[j] for j in range(2 * gbits)]
    is_row_src = [jnp.where(q[j] >= gbits, 1, 0) for j in range(2 * gbits)]
    crossing = [is_row_src[j] if j < gbits else 1 - is_row_src[j] for j in range(2 * gbits)]
    k = sum(crossing[:gbits])
    pos = []
    for group in range(2):
        n_cross = 0
        n_stay = 0
        for t in range(gbits):
            cr = crossing[group * gbits + t]
            pos.append(jnp.where(cr == 1, n_cross, k + n_stay))
            n_cross = n_cross + cr
            n_stay = n_stay + (1 - cr)
    lane = lax.broadcasted_iota(jnp.int32, (1, width), 1)
    row_to = jnp.zeros((1, width), jnp.int32)
    col_to = jnp.zeros((1, width), jnp.int32)
    for j in range(2 * gbits):
        bit = jnp.left_shift(jnp.right_shift(lane, q[j] - gbits * is_row_src[j]) & 1, pos[j])
        row_to = row_to + is_row_src[j] * bit
        col_to = col_to + (1 - is_row_src[j]) * bit
    row_from = jnp.zeros((1, width), jnp.int32)
    col_from = jnp.zeros((1, width), jnp.int32)
    for t in range(gbits):
        row_from = row_from + jnp.left_shift(jnp.right_shift(lane, t) & 1, pos[gbits + t])
        col_from = col_from + jnp.left_shift(jnp.right_shift(lane, t) & 1, pos[t])
    rows = lax.broadcasted_iota(jnp.int32, (width, width), 0)
    a = (rows == row_to).astype(F32)
    b_t = (rows == col_to).astype(F32)
    c_t = (rows == row_from).astype(F32)
    d = (rows == col_from).astype(F32)
    sr = s_ref[pl.ds(0, width, stride=2), :]
    si = s_ref[pl.ds(1, width, stride=2), :]
    x = mm(a, jnp.concatenate([sr, si], axis=1))
    x = mm_t(jnp.concatenate([x[:, :width], x[:, width:]], axis=0), b_t)
    rows2 = lax.broadcasted_iota(jnp.int32, (2 * width, width), 0)
    cols2 = lax.broadcasted_iota(jnp.int32, (2 * width, width), 1)
    for u in range(gbits):
        flipped = flip_bit(flip_bit(x, rows2, u, 0), cols2, u, 1)
        differ = (jnp.right_shift(rows2 ^ cols2, u) & 1) == 1
        x = jnp.where(differ & (u < k), flipped, x)
    h0 = mm_t(d, jnp.concatenate([g_ref[0, 0], g_ref[0, 1]], axis=0))
    h0r = h0[:, :width]
    h0i = h0[:, width:]
    u_ri = mm(jnp.concatenate([x[:width], x[width:]], axis=1), jnp.concatenate(
        [jnp.concatenate([h0r, h0i], axis=1), jnp.concatenate([-h0i, h0r], axis=1)], axis=0
    ))
    g1 = mm_t(jnp.concatenate([g_ref[1, 0], g_ref[1, 1]], axis=0), c_t)
    y = mm(complex_block(g1[:width], g1[width:]), jnp.concatenate([u_ri[:, :width], u_ri[:, width:]], axis=0))
    y_ref[pl.ds(0, width, stride=2), :] = y[:width]
    y_ref[pl.ds(1, width, stride=2), :] = y[width:]


def second_kernel(w_ref, g_ref, z_ref):
    width = g_ref.shape[-1]
    w = jnp.concatenate([w_ref[pl.ds(0, width, stride=2), :], w_ref[pl.ds(1, width, stride=2), :]], axis=0)
    v = mm(complex_block(g_ref[2, 0], g_ref[2, 1]), w)
    z = mm(complex_block(g_ref[3, 0], g_ref[3, 1]), v)
    z_ref[pl.ds(0, width, stride=2), :] = z[:width]
    z_ref[pl.ds(1, width, stride=2), :] = z[width:]


def exchange(y, width):
    parts = lax.axis_size("dev") * lax.axis_size("node")
    axes = ("dev", "node")
    if width % parts == 0:
        return lax.all_to_all(y, axes, 0, 0, tiled=True)
    split = parts // width
    v = y.reshape(width, 2, split, width // split).transpose(0, 2, 1, 3)
    v = lax.all_to_all(v.reshape(parts, -1), axes, 0, 0, tiled=True)
    v = v.reshape(width, split, 2, width // split).transpose(0, 2, 1, 3)
    return v.reshape(width, 2, width)


def local(state, gates, qubit_order):
    gbits = gates.shape[-1].bit_length() - 1
    width = 2**gbits
    rows = state.reshape(2, width, width).transpose(1, 0, 2).reshape(2 * width, width)
    y = pl.pallas_call(
        lambda *refs: first_kernel(*refs, gbits=gbits),
        out_shape=jax.ShapeDtypeStruct((2 * width, width), F32),
        grid=(1,),
        in_specs=[
            pl.BlockSpec(memory_space=pltpu.SMEM),
            pl.BlockSpec((2 * width, width), lambda i: (0, 0)),
            pl.BlockSpec((2, 2, width, width), lambda i: (0, 0, 0, 0)),
        ],
        out_specs=pl.BlockSpec((2 * width, width), lambda i: (0, 0)),
    )(qubit_order.astype(jnp.int32), rows, gates)
    w = exchange(y.reshape(width, 2, width), width).reshape(2 * width, width)
    z = pl.pallas_call(
        second_kernel,
        out_shape=jax.ShapeDtypeStruct((2 * width, width), F32),
        grid=(1,),
        in_specs=[
            pl.BlockSpec(memory_space=pltpu.VMEM),
            pl.BlockSpec(memory_space=pltpu.VMEM),
        ],
        out_specs=pl.BlockSpec((2 * width, width), lambda i: (0, 0)),
    )(pltpu.with_memory_space_constraint(w, pltpu.VMEM), pltpu.with_memory_space_constraint(gates, pltpu.VMEM))
    return z.reshape(width, 2, width).transpose(1, 0, 2).reshape(2, -1)


def solution(mesh):
    return jax.shard_map(
        local,
        mesh=mesh,
        in_specs=(P(None, ("node", "dev")), P(), P()),
        out_specs=P(None, ("node", "dev")),
        check_vma=False,
    )
```

```python
import jax
import jax.numpy as jnp
from jax import lax
from jax.experimental import pallas as pl
from jax.experimental.pallas import tpu as pltpu
from jax.sharding import PartitionSpec as P

HI = lax.Precision.HIGHEST
F32 = jnp.float32


def mm(a, b):
    return jnp.dot(a, b, precision=HI, preferred_element_type=F32)


def mm_t(a, b):
    return lax.dot_general(a, b, (((1,), (1,)), ((), ())), precision=HI, preferred_element_type=F32)


def flip_bit(x, index, u, axis):
    n = x.shape[axis]
    step = 2**u
    one = pltpu.roll(x, step, axis)
    other = pltpu.roll(x, n - step, axis)
    moved = pltpu.roll(index, step, axis)
    return jnp.where(moved == (index ^ step), one, other)


def complex_block(gr, gi):
    return jnp.concatenate(
        [jnp.concatenate([gr, -gi], axis=1), jnp.concatenate([gi, gr], axis=1)], axis=0
    )


def first_kernel(q_ref, s_ref, g_ref, y_ref, *, gbits):
    width = 2**gbits
    q = [q_ref[j] for j in range(2 * gbits)]
    is_row_src = [jnp.where(q[j] >= gbits, 1, 0) for j in range(2 * gbits)]
    crossing = [is_row_src[j] if j < gbits else 1 - is_row_src[j] for j in range(2 * gbits)]
    k = sum(crossing[:gbits])
    pos = []
    for group in range(2):
        n_cross = 0
        n_stay = 0
        for t in range(gbits):
            cr = crossing[group * gbits + t]
            pos.append(jnp.where(cr == 1, n_cross, k + n_stay))
            n_cross = n_cross + cr
            n_stay = n_stay + (1 - cr)
    lane = lax.broadcasted_iota(jnp.int32, (1, width), 1)
    row_to = jnp.zeros((1, width), jnp.int32)
    col_to = jnp.zeros((1, width), jnp.int32)
    for j in range(2 * gbits):
        bit = jnp.left_shift(jnp.right_shift(lane, q[j] - gbits * is_row_src[j]) & 1, pos[j])
        row_to = row_to + is_row_src[j] * bit
        col_to = col_to + (1 - is_row_src[j]) * bit
    row_from = jnp.zeros((1, width), jnp.int32)
    col_from = jnp.zeros((1, width), jnp.int32)
    for t in range(gbits):
        row_from = row_from + jnp.left_shift(jnp.right_shift(lane, t) & 1, pos[gbits + t])
        col_from = col_from + jnp.left_shift(jnp.right_shift(lane, t) & 1, pos[t])
    rows = lax.broadcasted_iota(jnp.int32, (width, width), 0)
    a = (rows == row_to).astype(F32)
    b_t = (rows == col_to).astype(F32)
    c_t = (rows == row_from).astype(F32)
    d = (rows == col_from).astype(F32)
    sr = s_ref[pl.ds(0, width, stride=2), :]
    si = s_ref[pl.ds(1, width, stride=2), :]
    x = mm(a, jnp.concatenate([sr, si], axis=1))
    x = mm_t(jnp.concatenate([x[:, :width], x[:, width:]], axis=0), b_t)
    rows2 = lax.broadcasted_iota(jnp.int32, (2 * width, width), 0)
    cols2 = lax.broadcasted_iota(jnp.int32, (2 * width, width), 1)
    for u in range(gbits):
        flipped = flip_bit(flip_bit(x, rows2, u, 0), cols2, u, 1)
        differ = (jnp.right_shift(rows2 ^ cols2, u) & 1) == 1
        x = jnp.where(differ & (u < k), flipped, x)
    h0 = mm_t(d, jnp.concatenate([g_ref[0, 0], g_ref[0, 1]], axis=0))
    h0r = h0[:, :width]
    h0i = h0[:, width:]
    u_ri = mm(jnp.concatenate([x[:width], x[width:]], axis=1), jnp.concatenate(
        [jnp.concatenate([h0r, h0i], axis=1), jnp.concatenate([-h0i, h0r], axis=1)], axis=0
    ))
    g1 = mm_t(jnp.concatenate([g_ref[1, 0], g_ref[1, 1]], axis=0), c_t)
    y = mm(complex_block(g1[:width], g1[width:]), jnp.concatenate([u_ri[:, :width], u_ri[:, width:]], axis=0))
    y_ref[pl.ds(0, width, stride=2), :] = y[:width]
    y_ref[pl.ds(1, width, stride=2), :] = y[width:]


def second_kernel(w_ref, g_ref, z_ref):
    width = g_ref.shape[-1]
    w = jnp.concatenate([w_ref[pl.ds(0, width, stride=2), :], w_ref[pl.ds(1, width, stride=2), :]], axis=0)
    v = mm(complex_block(g_ref[2, 0], g_ref[2, 1]), w)
    z = mm(complex_block(g_ref[3, 0], g_ref[3, 1]), v)
    z_ref[pl.ds(0, width, stride=2), :] = z[:width]
    z_ref[pl.ds(1, width, stride=2), :] = z[width:]


def exchange(y, width):
    parts = lax.axis_size("dev") * lax.axis_size("node")
    axes = ("dev", "node")
    if width % parts == 0:
        return lax.all_to_all(y, axes, 0, 0, tiled=True)
    split = parts // width
    v = y.reshape(width, 2, split, width // split).transpose(0, 2, 1, 3)
    v = lax.all_to_all(v.reshape(parts, -1), axes, 0, 0, tiled=True)
    v = v.reshape(width, split, 2, width // split).transpose(0, 2, 1, 3)
    return v.reshape(width, 2, width)


def local(state, gates, qubit_order):
    gbits = gates.shape[-1].bit_length() - 1
    width = 2**gbits
    rows = state.reshape(2, width, width).transpose(1, 0, 2).reshape(2 * width, width)
    y = pl.pallas_call(
        lambda *refs: first_kernel(*refs, gbits=gbits),
        out_shape=pltpu.VMEM((2 * width, width), F32),
        grid=(1,),
        in_specs=[
            pl.BlockSpec(memory_space=pltpu.SMEM),
            pl.BlockSpec((2 * width, width), lambda i: (0, 0)),
            pl.BlockSpec((2, 2, width, width), lambda i: (0, 0, 0, 0)),
        ],
        out_specs=pl.BlockSpec(memory_space=pltpu.VMEM),
    )(qubit_order.astype(jnp.int32), rows, gates)
    w = exchange(y.reshape(width, 2, width), width).reshape(2 * width, width)
    z = pl.pallas_call(
        second_kernel,
        out_shape=jax.ShapeDtypeStruct((2 * width, width), F32),
        grid=(1,),
        in_specs=[
            pl.BlockSpec(memory_space=pltpu.VMEM),
            pl.BlockSpec(memory_space=pltpu.VMEM),
        ],
        out_specs=pl.BlockSpec((2 * width, width), lambda i: (0, 0)),
    )(pltpu.with_memory_space_constraint(w, pltpu.VMEM), pltpu.with_memory_space_constraint(gates, pltpu.VMEM))
    return z.reshape(width, 2, width).transpose(1, 0, 2).reshape(2, -1)


def solution(mesh):
    return jax.shard_map(
        local,
        mesh=mesh,
        in_specs=(P(None, ("node", "dev")), P(), P()),
        out_specs=P(None, ("node", "dev")),
        check_vma=False,
    )
```

```python
import jax
import jax.numpy as jnp
from jax import lax
from jax.experimental import pallas as pl
from jax.experimental.pallas import tpu as pltpu
from jax.sharding import PartitionSpec as P

HI = lax.Precision.HIGHEST
F32 = jnp.float32


def mm(a, b):
    return jnp.dot(a, b, precision=HI, preferred_element_type=F32)


def mm_t(a, b):
    return lax.dot_general(a, b, (((1,), (1,)), ((), ())), precision=HI, preferred_element_type=F32)


def flip_bit(x, index, u, axis):
    n = x.shape[axis]
    step = 2**u
    one = pltpu.roll(x, step, axis)
    other = pltpu.roll(x, n - step, axis)
    moved = pltpu.roll(index, step, axis)
    return jnp.where(moved == (index ^ step), one, other)


def complex_block(gr, gi):
    return jnp.concatenate(
        [jnp.concatenate([gr, -gi], axis=1), jnp.concatenate([gi, gr], axis=1)], axis=0
    )


def first_kernel(q_ref, s_ref, g_ref, y_ref, x_ref, pair_ref, *, gbits):
    width = 2**gbits
    q = [q_ref[j] for j in range(2 * gbits)]
    for slot in range(2 * (gbits + 1)):
        pair_ref[slot] = gbits
    rank_col = 0
    rank_row = 0
    for t in range(gbits):
        col_cross = q[t] >= gbits
        row_cross = q[gbits + t] < gbits
        pair_ref[jnp.where(col_cross, rank_col, gbits)] = q[t] - gbits
        pair_ref[gbits + 1 + jnp.where(row_cross, rank_row, gbits)] = q[gbits + t]
        rank_col = rank_col + jnp.where(col_cross, 1, 0)
        rank_row = rank_row + jnp.where(row_cross, 1, 0)
    row_of = [pair_ref[i] for i in range(gbits)]
    col_of = [pair_ref[gbits + 1 + i] for i in range(gbits)]
    partner = [gbits] * gbits
    partner_back = [gbits] * gbits
    for i in range(gbits):
        for a in range(gbits):
            partner[a] = jnp.where(row_of[i] == a, col_of[i], partner[a])
            partner_back[a] = jnp.where(col_of[i] == a, row_of[i], partner_back[a])
    pos = []
    for j in range(2 * gbits):
        src = q[j] - gbits if j < gbits else q[j]
        moved = src
        for a in range(gbits):
            moved = jnp.where(src == a, partner[a] if j < gbits else partner_back[a], moved)
        if j < gbits:
            pos.append(jnp.where(q[j] >= gbits, moved, q[j]))
        else:
            pos.append(jnp.where(q[j] < gbits, moved, q[j] - gbits))
    lane = lax.broadcasted_iota(jnp.int32, (1, width), 1)
    row_from = jnp.zeros((1, width), jnp.int32)
    col_from = jnp.zeros((1, width), jnp.int32)
    for t in range(gbits):
        row_from = row_from + jnp.left_shift(jnp.right_shift(lane, t) & 1, pos[gbits + t])
        col_from = col_from + jnp.left_shift(jnp.right_shift(lane, t) & 1, pos[t])
    rows = lax.broadcasted_iota(jnp.int32, (width, width), 0)
    c_t = (rows == row_from).astype(F32)
    d = (rows == col_from).astype(F32)
    x_ref[...] = jnp.concatenate(
        [s_ref[pl.ds(0, width, stride=2), :], s_ref[pl.ds(1, width, stride=2), :]], axis=0
    )
    for a in range(gbits):
        b = partner[a]

        @pl.when(b < gbits)
        def _():
            rows2 = lax.broadcasted_iota(jnp.int32, (2 * width, width), 0)
            cols2 = lax.broadcasted_iota(jnp.int32, (2 * width, width), 1)
            held = x_ref[...]
            step = jnp.left_shift(1, b)
            one = pltpu.roll(held, step, 1)
            other = pltpu.roll(held, width - step, 1)
            turned = pltpu.roll(cols2, step, 1)
            flipped = jnp.where(turned == (cols2 ^ step), one, other)
            flipped = flip_bit(flipped, rows2, a, 0)
            differ = ((jnp.right_shift(rows2, a) ^ jnp.right_shift(cols2, b)) & 1) == 1
            x_ref[...] = jnp.where(differ, flipped, held)

    x = x_ref[...]
    h0 = mm_t(d, jnp.concatenate([g_ref[0, 0], g_ref[0, 1]], axis=0))
    h0r = h0[:, :width]
    h0i = h0[:, width:]
    u_ri = mm(jnp.concatenate([x[:width], x[width:]], axis=1), jnp.concatenate(
        [jnp.concatenate([h0r, h0i], axis=1), jnp.concatenate([-h0i, h0r], axis=1)], axis=0
    ))
    g1 = mm_t(jnp.concatenate([g_ref[1, 0], g_ref[1, 1]], axis=0), c_t)
    y = mm(complex_block(g1[:width], g1[width:]), jnp.concatenate([u_ri[:, :width], u_ri[:, width:]], axis=0))
    y_ref[pl.ds(0, width, stride=2), :] = y[:width]
    y_ref[pl.ds(1, width, stride=2), :] = y[width:]


def second_kernel(w_ref, g_ref, z_ref):
    width = g_ref.shape[-1]
    w = jnp.concatenate([w_ref[pl.ds(0, width, stride=2), :], w_ref[pl.ds(1, width, stride=2), :]], axis=0)
    v = mm(complex_block(g_ref[2, 0], g_ref[2, 1]), w)
    z = mm(complex_block(g_ref[3, 0], g_ref[3, 1]), v)
    z_ref[pl.ds(0, width, stride=2), :] = z[:width]
    z_ref[pl.ds(1, width, stride=2), :] = z[width:]


def exchange(y, width):
    parts = lax.axis_size("dev") * lax.axis_size("node")
    axes = ("dev", "node")
    if width % parts == 0:
        return lax.all_to_all(y, axes, 0, 0, tiled=True)
    split = parts // width
    v = y.reshape(width, 2, split, width // split).transpose(0, 2, 1, 3)
    v = lax.all_to_all(v.reshape(parts, -1), axes, 0, 0, tiled=True)
    v = v.reshape(width, split, 2, width // split).transpose(0, 2, 1, 3)
    return v.reshape(width, 2, width)


def local(state, gates, qubit_order):
    gbits = gates.shape[-1].bit_length() - 1
    width = 2**gbits
    rows = state.reshape(2, width, width).transpose(1, 0, 2).reshape(2 * width, width)
    y = pl.pallas_call(
        lambda *refs: first_kernel(*refs, gbits=gbits),
        out_shape=pltpu.VMEM((2 * width, width), F32),
        grid=(1,),
        in_specs=[
            pl.BlockSpec(memory_space=pltpu.SMEM),
            pl.BlockSpec((2 * width, width), lambda i: (0, 0)),
            pl.BlockSpec((2, 2, width, width), lambda i: (0, 0, 0, 0)),
        ],
        out_specs=pl.BlockSpec(memory_space=pltpu.VMEM),
        scratch_shapes=[pltpu.VMEM((2 * width, width), F32), pltpu.SMEM((2 * (gbits + 1),), jnp.int32)],
    )(qubit_order.astype(jnp.int32), rows, gates)
    w = exchange(y.reshape(width, 2, width), width).reshape(2 * width, width)
    z = pl.pallas_call(
        second_kernel,
        out_shape=jax.ShapeDtypeStruct((2 * width, width), F32),
        grid=(1,),
        in_specs=[
            pl.BlockSpec(memory_space=pltpu.VMEM),
            pl.BlockSpec(memory_space=pltpu.VMEM),
        ],
        out_specs=pl.BlockSpec((2 * width, width), lambda i: (0, 0)),
    )(pltpu.with_memory_space_constraint(w, pltpu.VMEM), pltpu.with_memory_space_constraint(gates, pltpu.VMEM))
    return z.reshape(width, 2, width).transpose(1, 0, 2).reshape(2, -1)


def solution(mesh):
    return jax.shard_map(
        local,
        mesh=mesh,
        in_specs=(P(None, ("node", "dev")), P(), P()),
        out_specs=P(None, ("node", "dev")),
        check_vma=False,
    )
```

```python
import jax
import jax.numpy as jnp
from jax import lax
from jax.experimental import pallas as pl
from jax.experimental.pallas import tpu as pltpu
from jax.sharding import PartitionSpec as P

HI = lax.Precision.HIGHEST
F32 = jnp.float32


def mm(a, b):
    return jnp.dot(a, b, precision=HI, preferred_element_type=F32)


def mm_t(a, b):
    return lax.dot_general(a, b, (((1,), (1,)), ((), ())), precision=HI, preferred_element_type=F32)


def flip_bit(x, index, u, axis):
    n = x.shape[axis]
    step = 2**u
    one = pltpu.roll(x, step, axis)
    other = pltpu.roll(x, n - step, axis)
    moved = pltpu.roll(index, step, axis)
    return jnp.where(moved == (index ^ step), one, other)


def complex_block(gr, gi):
    return jnp.concatenate(
        [jnp.concatenate([gr, -gi], axis=1), jnp.concatenate([gi, gr], axis=1)], axis=0
    )


def first_kernel(q_ref, s_ref, g_ref, y_ref, x_ref, pair_ref, *, gbits):
    width = 2**gbits
    q = [q_ref[j] for j in range(2 * gbits)]
    for slot in range(2 * (gbits + 1)):
        pair_ref[slot] = gbits
    rank_col = 0
    rank_row = 0
    for t in range(gbits):
        col_cross = q[t] >= gbits
        row_cross = q[gbits + t] < gbits
        pair_ref[jnp.where(col_cross, rank_col, gbits)] = q[t] - gbits
        pair_ref[gbits + 1 + jnp.where(row_cross, rank_row, gbits)] = q[gbits + t]
        rank_col = rank_col + jnp.where(col_cross, 1, 0)
        rank_row = rank_row + jnp.where(row_cross, 1, 0)
    row_of = [pair_ref[i] for i in range(gbits)]
    col_of = [pair_ref[gbits + 1 + i] for i in range(gbits)]
    partner = [gbits] * gbits
    partner_back = [gbits] * gbits
    for i in range(gbits):
        for a in range(gbits):
            partner[a] = jnp.where(row_of[i] == a, col_of[i], partner[a])
            partner_back[a] = jnp.where(col_of[i] == a, row_of[i], partner_back[a])
    row_cross = [partner[u] < gbits for u in range(gbits)]
    col_cross = [partner_back[u] < gbits for u in range(gbits)]
    held_at = 0
    for u in range(gbits):
        pair_ref[jnp.where(row_cross[u], gbits, held_at)] = u
        held_at = held_at + jnp.where(row_cross[u], 0, 1)
    kept = [pair_ref[u] for u in range(gbits)]
    col_pos = []
    stay_rank = 0
    for u in range(gbits):
        free = kept[0]
        for r in range(1, gbits):
            free = jnp.where(stay_rank == r, kept[r], free)
        col_pos.append(jnp.where(col_cross[u], partner_back[u], free))
        stay_rank = stay_rank + jnp.where(col_cross[u], 0, 1)
    pos = []
    for j in range(2 * gbits):
        if j < gbits:
            src_col = col_pos[0]
            for u in range(1, gbits):
                src_col = jnp.where(q[j] == u, col_pos[u], src_col)
            pos.append(jnp.where(q[j] >= gbits, q[j] - gbits, src_col))
        else:
            back = partner_back[0]
            for u in range(1, gbits):
                back = jnp.where(q[j] == u, partner_back[u], back)
            pos.append(jnp.where(q[j] < gbits, back, q[j] - gbits))
    lane = lax.broadcasted_iota(jnp.int32, (1, width), 1)
    col_to = jnp.zeros((1, width), jnp.int32)
    row_from = jnp.zeros((1, width), jnp.int32)
    col_from = jnp.zeros((1, width), jnp.int32)
    for t in range(gbits):
        col_to = col_to + jnp.left_shift(jnp.right_shift(lane, t) & 1, col_pos[t])
        row_from = row_from + jnp.left_shift(jnp.right_shift(lane, t) & 1, pos[gbits + t])
        col_from = col_from + jnp.left_shift(jnp.right_shift(lane, t) & 1, pos[t])
    rows = lax.broadcasted_iota(jnp.int32, (width, width), 0)
    b_t = (rows == col_to).astype(F32)
    c_t = (rows == row_from).astype(F32)
    d = (rows == col_from).astype(F32)
    x = jnp.concatenate(
        [s_ref[pl.ds(0, width, stride=2), :], s_ref[pl.ds(1, width, stride=2), :]], axis=0
    )
    x = mm_t(x, b_t)
    rows2 = lax.broadcasted_iota(jnp.int32, (2 * width, width), 0)
    cols2 = lax.broadcasted_iota(jnp.int32, (2 * width, width), 1)
    for u in range(gbits):
        flipped = flip_bit(flip_bit(x, rows2, u, 0), cols2, u, 1)
        differ = (jnp.right_shift(rows2 ^ cols2, u) & 1) == 1
        x = jnp.where(differ & row_cross[u], flipped, x)
    x_ref[...] = x
    x = x_ref[...]
    h0 = mm_t(d, jnp.concatenate([g_ref[0, 0], g_ref[0, 1]], axis=0))
    h0r = h0[:, :width]
    h0i = h0[:, width:]
    u_ri = mm(jnp.concatenate([x[:width], x[width:]], axis=1), jnp.concatenate(
        [jnp.concatenate([h0r, h0i], axis=1), jnp.concatenate([-h0i, h0r], axis=1)], axis=0
    ))
    g1 = mm_t(jnp.concatenate([g_ref[1, 0], g_ref[1, 1]], axis=0), c_t)
    y = mm(complex_block(g1[:width], g1[width:]), jnp.concatenate([u_ri[:, :width], u_ri[:, width:]], axis=0))
    y_ref[pl.ds(0, width, stride=2), :] = y[:width]
    y_ref[pl.ds(1, width, stride=2), :] = y[width:]


def second_kernel(w_ref, g_ref, z_ref):
    width = g_ref.shape[-1]
    w = jnp.concatenate([w_ref[pl.ds(0, width, stride=2), :], w_ref[pl.ds(1, width, stride=2), :]], axis=0)
    v = mm(complex_block(g_ref[2, 0], g_ref[2, 1]), w)
    z = mm(complex_block(g_ref[3, 0], g_ref[3, 1]), v)
    z_ref[pl.ds(0, width, stride=2), :] = z[:width]
    z_ref[pl.ds(1, width, stride=2), :] = z[width:]


def exchange(y, width):
    parts = lax.axis_size("dev") * lax.axis_size("node")
    axes = ("dev", "node")
    if width % parts == 0:
        return lax.all_to_all(y, axes, 0, 0, tiled=True)
    split = parts // width
    v = y.reshape(width, 2, split, width // split).transpose(0, 2, 1, 3)
    v = lax.all_to_all(v.reshape(parts, -1), axes, 0, 0, tiled=True)
    v = v.reshape(width, split, 2, width // split).transpose(0, 2, 1, 3)
    return v.reshape(width, 2, width)


def local(state, gates, qubit_order):
    gbits = gates.shape[-1].bit_length() - 1
    width = 2**gbits
    rows = state.reshape(2, width, width).transpose(1, 0, 2).reshape(2 * width, width)
    y = pl.pallas_call(
        lambda *refs: first_kernel(*refs, gbits=gbits),
        out_shape=pltpu.VMEM((2 * width, width), F32),
        grid=(1,),
        in_specs=[
            pl.BlockSpec(memory_space=pltpu.SMEM),
            pl.BlockSpec((2 * width, width), lambda i: (0, 0)),
            pl.BlockSpec((2, 2, width, width), lambda i: (0, 0, 0, 0)),
        ],
        out_specs=pl.BlockSpec(memory_space=pltpu.VMEM),
        scratch_shapes=[pltpu.VMEM((2 * width, width), F32), pltpu.SMEM((2 * (gbits + 1),), jnp.int32)],
    )(qubit_order.astype(jnp.int32), rows, gates)
    w = exchange(y.reshape(width, 2, width), width).reshape(2 * width, width)
    z = pl.pallas_call(
        second_kernel,
        out_shape=jax.ShapeDtypeStruct((2 * width, width), F32),
        grid=(1,),
        in_specs=[
            pl.BlockSpec(memory_space=pltpu.VMEM),
            pl.BlockSpec(memory_space=pltpu.VMEM),
        ],
        out_specs=pl.BlockSpec((2 * width, width), lambda i: (0, 0)),
    )(pltpu.with_memory_space_constraint(w, pltpu.VMEM), pltpu.with_memory_space_constraint(gates, pltpu.VMEM))
    return z.reshape(width, 2, width).transpose(1, 0, 2).reshape(2, -1)


def solution(mesh):
    return jax.shard_map(
        local,
        mesh=mesh,
        in_specs=(P(None, ("node", "dev")), P(), P()),
        out_specs=P(None, ("node", "dev")),
        check_vma=False,
    )
```

```python
import jax
import jax.numpy as jnp
from jax import lax
from jax.experimental import pallas as pl
from jax.experimental.pallas import tpu as pltpu
from jax.sharding import PartitionSpec as P

HI = lax.Precision.HIGHEST
F32 = jnp.float32


def mm(a, b):
    return jnp.dot(a, b, precision=HI, preferred_element_type=F32)


def mm_t(a, b):
    return lax.dot_general(a, b, (((1,), (1,)), ((), ())), precision=HI, preferred_element_type=F32)


def flip_bit(x, index, u, axis):
    n = x.shape[axis]
    step = 2**u
    one = pltpu.roll(x, step, axis)
    other = pltpu.roll(x, n - step, axis)
    moved = pltpu.roll(index, step, axis)
    return jnp.where(moved == (index ^ step), one, other)


def complex_block(gr, gi):
    return jnp.concatenate(
        [jnp.concatenate([gr, -gi], axis=1), jnp.concatenate([gi, gr], axis=1)], axis=0
    )


def first_kernel(q_ref, s_ref, g_ref, h_ref, y_ref, m_ref, x_ref, pair_ref, *, gbits, order):
    width = 2**gbits
    q = [q_ref[j] for j in range(2 * gbits)]
    for slot in range(2 * (gbits + 1)):
        pair_ref[slot] = gbits
    rank_col = 0
    rank_row = 0
    for t in range(gbits):
        col_cross = q[t] >= gbits
        row_cross = q[gbits + t] < gbits
        pair_ref[jnp.where(col_cross, rank_col, gbits)] = q[t] - gbits
        pair_ref[gbits + 1 + jnp.where(row_cross, rank_row, gbits)] = q[gbits + t]
        rank_col = rank_col + jnp.where(col_cross, 1, 0)
        rank_row = rank_row + jnp.where(row_cross, 1, 0)
    row_of = [pair_ref[i] for i in range(gbits)]
    col_of = [pair_ref[gbits + 1 + i] for i in range(gbits)]
    partner = [gbits] * gbits
    partner_back = [gbits] * gbits
    for i in range(gbits):
        for a in range(gbits):
            partner[a] = jnp.where(row_of[i] == a, col_of[i], partner[a])
            partner_back[a] = jnp.where(col_of[i] == a, row_of[i], partner_back[a])
    row_cross = [partner[u] < gbits for u in range(gbits)]
    col_cross = [partner_back[u] < gbits for u in range(gbits)]
    held_at = 0
    for u in range(gbits):
        pair_ref[jnp.where(row_cross[u], gbits, held_at)] = u
        held_at = held_at + jnp.where(row_cross[u], 0, 1)
    kept = [pair_ref[u] for u in range(gbits)]
    col_pos = []
    stay_rank = 0
    for u in range(gbits):
        free = kept[0]
        for r in range(1, gbits):
            free = jnp.where(stay_rank == r, kept[r], free)
        col_pos.append(jnp.where(col_cross[u], partner_back[u], free))
        stay_rank = stay_rank + jnp.where(col_cross[u], 0, 1)
    pos = []
    for j in range(2 * gbits):
        if j < gbits:
            src_col = col_pos[0]
            for u in range(1, gbits):
                src_col = jnp.where(q[j] == u, col_pos[u], src_col)
            pos.append(jnp.where(q[j] >= gbits, q[j] - gbits, src_col))
        else:
            back = partner_back[0]
            for u in range(1, gbits):
                back = jnp.where(q[j] == u, partner_back[u], back)
            pos.append(jnp.where(q[j] < gbits, back, q[j] - gbits))
    lane = lax.broadcasted_iota(jnp.int32, (1, width), 1)
    col_to = jnp.zeros((1, width), jnp.int32)
    row_from = jnp.zeros((1, width), jnp.int32)
    col_from = jnp.zeros((1, width), jnp.int32)
    for t in range(gbits):
        col_to = col_to + jnp.left_shift(jnp.right_shift(lane, t) & 1, col_pos[t])
        row_from = row_from + jnp.left_shift(jnp.right_shift(lane, t) & 1, pos[gbits + t])
        col_from = col_from + jnp.left_shift(jnp.right_shift(lane, t) & 1, pos[t])
    rows = lax.broadcasted_iota(jnp.int32, (width, width), 0)
    b_t = (rows == col_to).astype(F32)
    c_t = (rows == row_from).astype(F32)
    d = (rows == col_from).astype(F32)
    x = jnp.concatenate(
        [s_ref[pl.ds(0, width, stride=2), :], s_ref[pl.ds(1, width, stride=2), :]], axis=0
    )
    x = mm_t(x, b_t)
    rows2 = lax.broadcasted_iota(jnp.int32, (2 * width, width), 0)
    cols2 = lax.broadcasted_iota(jnp.int32, (2 * width, width), 1)
    for u in range(gbits):
        flipped = flip_bit(flip_bit(x, rows2, u, 0), cols2, u, 1)
        differ = (jnp.right_shift(rows2 ^ cols2, u) & 1) == 1
        x = jnp.where(differ & row_cross[u], flipped, x)
    x_ref[...] = x
    x = x_ref[...]
    h0 = mm_t(d, jnp.concatenate([g_ref[0, 0], g_ref[0, 1]], axis=0))
    h0r = h0[:, :width]
    h0i = h0[:, width:]
    u_ri = mm(jnp.concatenate([x[:width], x[width:]], axis=1), jnp.concatenate(
        [jnp.concatenate([h0r, h0i], axis=1), jnp.concatenate([-h0i, h0r], axis=1)], axis=0
    ))
    g1_rows = []
    for p in range(2):
        g1_rows += [g_ref[1, p, pl.ds(start, size), :] for start, size in order]
    g1 = mm_t(jnp.concatenate(g1_rows, axis=0), c_t)
    cols = lax.broadcasted_iota(jnp.int32, (width, width), 1)
    taken = jnp.zeros((width, width), jnp.int32)
    at = 0
    for start, size in order:
        inside = (cols >= at) & (cols < at + size)
        taken = jnp.where(inside, cols - at + start, taken)
        at += size
    arrive = (rows == taken).astype(F32)
    g2 = mm(jnp.concatenate([h_ref[0, 0], h_ref[0, 1]], axis=0), arrive)
    m_ref[...] = mm(complex_block(h_ref[1, 0], h_ref[1, 1]), g2)
    y = mm(complex_block(g1[:width], g1[width:]), jnp.concatenate([u_ri[:, :width], u_ri[:, width:]], axis=0))
    y_ref[pl.ds(0, width, stride=2), :] = y[:width]
    y_ref[pl.ds(1, width, stride=2), :] = y[width:]


def second_kernel(w_ref, m_ref, z_ref):
    width = m_ref.shape[-1]
    w = jnp.concatenate([w_ref[pl.ds(0, width, stride=2), :], w_ref[pl.ds(1, width, stride=2), :]], axis=0)
    z = mm(complex_block(m_ref[:width], m_ref[width:]), w)
    z_ref[pl.ds(0, width, stride=2), :] = z[:width]
    z_ref[pl.ds(1, width, stride=2), :] = z[width:]


def send_order(width):
    n_node = lax.axis_size("node")
    n_dev = lax.axis_size("dev")
    size = width // (n_node * n_dev)
    return tuple(((m // n_dev + n_node * (m % n_dev)) * size, size) for m in range(n_node * n_dev))


def exchange(y, width):
    parts = lax.axis_size("dev") * lax.axis_size("node")
    if width % parts == 0:
        return lax.all_to_all(y, ("node", "dev"), 0, 0, tiled=True)
    axes = ("dev", "node")
    split = parts // width
    v = y.reshape(width, 2, split, width // split).transpose(0, 2, 1, 3)
    v = lax.all_to_all(v.reshape(parts, -1), axes, 0, 0, tiled=True)
    v = v.reshape(width, split, 2, width // split).transpose(0, 2, 1, 3)
    return v.reshape(width, 2, width)


def local(state, gates, qubit_order):
    gbits = gates.shape[-1].bit_length() - 1
    width = 2**gbits
    parts = lax.axis_size("dev") * lax.axis_size("node")
    if width % parts == 0:
        order = send_order(width)
    else:
        order = ((0, width),)
    rows = state.reshape(2, width, width).transpose(1, 0, 2).reshape(2 * width, width)
    vmem = pl.BlockSpec(memory_space=pltpu.VMEM)
    y, m = pl.pallas_call(
        lambda *refs: first_kernel(*refs, gbits=gbits, order=order),
        out_shape=(pltpu.VMEM((2 * width, width), F32), pltpu.VMEM((2 * width, width), F32)),
        grid=(1,),
        in_specs=[
            pl.BlockSpec(memory_space=pltpu.SMEM),
            pl.BlockSpec((2 * width, width), lambda i: (0, 0)),
            pl.BlockSpec((2, 2, width, width), lambda i: (0, 0, 0, 0)),
            pl.BlockSpec((2, 2, width, width), lambda i: (1, 0, 0, 0)),
        ],
        out_specs=(vmem, vmem),
        scratch_shapes=[pltpu.VMEM((2 * width, width), F32), pltpu.SMEM((2 * (gbits + 1),), jnp.int32)],
    )(qubit_order.astype(jnp.int32), rows, gates, gates)
    w = exchange(y.reshape(width, 2, width), width).reshape(2 * width, width)
    z = pl.pallas_call(
        second_kernel,
        out_shape=jax.ShapeDtypeStruct((2 * width, width), F32),
        in_specs=[vmem, vmem],
        out_specs=pl.BlockSpec(memory_space=pltpu.VMEM),
    )(pltpu.with_memory_space_constraint(w, pltpu.VMEM), pltpu.with_memory_space_constraint(m, pltpu.VMEM))
    return z.reshape(width, 2, width).transpose(1, 0, 2).reshape(2, -1)


def solution(mesh):
    return jax.shard_map(
        local,
        mesh=mesh,
        in_specs=(P(None, ("node", "dev")), P(), P()),
        out_specs=P(None, ("node", "dev")),
        check_vma=False,
    )
```

```python
import jax
import jax.numpy as jnp
from jax import lax
from jax.experimental import pallas as pl
from jax.experimental.pallas import tpu as pltpu
from jax.sharding import PartitionSpec as P

HI = lax.Precision.HIGHEST
F32 = jnp.float32


def mm(a, b):
    return jnp.dot(a, b, precision=HI, preferred_element_type=F32)


def mm_t(a, b, precision=HI):
    return lax.dot_general(a, b, (((1,), (1,)), ((), ())), precision=precision, preferred_element_type=F32)


PICK = lax.Precision.HIGH


def flip_bit(x, index, u, axis):
    n = x.shape[axis]
    step = 2**u
    one = pltpu.roll(x, step, axis)
    other = pltpu.roll(x, n - step, axis)
    moved = pltpu.roll(index, step, axis)
    return jnp.where(moved == (index ^ step), one, other)


def complex_block(gr, gi):
    return jnp.concatenate(
        [jnp.concatenate([gr, -gi], axis=1), jnp.concatenate([gi, gr], axis=1)], axis=0
    )


def first_kernel(q_ref, s_ref, g_ref, h_ref, y_ref, m_ref, x_ref, pair_ref, *, gbits, order):
    width = 2**gbits
    q = [q_ref[j] for j in range(2 * gbits)]
    for slot in range(2 * (gbits + 1)):
        pair_ref[slot] = gbits
    rank_col = 0
    rank_row = 0
    for t in range(gbits):
        col_cross = q[t] >= gbits
        row_cross = q[gbits + t] < gbits
        pair_ref[jnp.where(col_cross, rank_col, gbits)] = q[t] - gbits
        pair_ref[gbits + 1 + jnp.where(row_cross, rank_row, gbits)] = q[gbits + t]
        rank_col = rank_col + jnp.where(col_cross, 1, 0)
        rank_row = rank_row + jnp.where(row_cross, 1, 0)
    row_of = [pair_ref[i] for i in range(gbits)]
    col_of = [pair_ref[gbits + 1 + i] for i in range(gbits)]
    partner = [gbits] * gbits
    partner_back = [gbits] * gbits
    for i in range(gbits):
        for a in range(gbits):
            partner[a] = jnp.where(row_of[i] == a, col_of[i], partner[a])
            partner_back[a] = jnp.where(col_of[i] == a, row_of[i], partner_back[a])
    row_cross = [partner[u] < gbits for u in range(gbits)]
    col_cross = [partner_back[u] < gbits for u in range(gbits)]
    held_at = 0
    for u in range(gbits):
        pair_ref[jnp.where(row_cross[u], gbits, held_at)] = u
        held_at = held_at + jnp.where(row_cross[u], 0, 1)
    kept = [pair_ref[u] for u in range(gbits)]
    col_pos = []
    stay_rank = 0
    for u in range(gbits):
        free = kept[0]
        for r in range(1, gbits):
            free = jnp.where(stay_rank == r, kept[r], free)
        col_pos.append(jnp.where(col_cross[u], partner_back[u], free))
        stay_rank = stay_rank + jnp.where(col_cross[u], 0, 1)
    pos = []
    for j in range(2 * gbits):
        if j < gbits:
            src_col = col_pos[0]
            for u in range(1, gbits):
                src_col = jnp.where(q[j] == u, col_pos[u], src_col)
            pos.append(jnp.where(q[j] >= gbits, q[j] - gbits, src_col))
        else:
            back = partner_back[0]
            for u in range(1, gbits):
                back = jnp.where(q[j] == u, partner_back[u], back)
            pos.append(jnp.where(q[j] < gbits, back, q[j] - gbits))
    lane = lax.broadcasted_iota(jnp.int32, (1, width), 1)
    col_to = jnp.zeros((1, width), jnp.int32)
    row_from = jnp.zeros((1, width), jnp.int32)
    col_from = jnp.zeros((1, width), jnp.int32)
    for t in range(gbits):
        col_to = col_to + jnp.left_shift(jnp.right_shift(lane, t) & 1, col_pos[t])
        row_from = row_from + jnp.left_shift(jnp.right_shift(lane, t) & 1, pos[gbits + t])
        col_from = col_from + jnp.left_shift(jnp.right_shift(lane, t) & 1, pos[t])
    rows = lax.broadcasted_iota(jnp.int32, (width, width), 0)
    b_t = (rows == col_to).astype(F32)
    c_t = (rows == row_from).astype(F32)
    d = (rows == col_from).astype(F32)
    x = jnp.concatenate(
        [s_ref[pl.ds(0, width, stride=2), :], s_ref[pl.ds(1, width, stride=2), :]], axis=0
    )
    x = mm_t(x, b_t, PICK)
    rows2 = lax.broadcasted_iota(jnp.int32, (2 * width, width), 0)
    cols2 = lax.broadcasted_iota(jnp.int32, (2 * width, width), 1)
    for u in range(gbits):
        flipped = flip_bit(flip_bit(x, rows2, u, 0), cols2, u, 1)
        differ = (jnp.right_shift(rows2 ^ cols2, u) & 1) == 1
        x = jnp.where(differ & row_cross[u], flipped, x)
    x_ref[...] = x
    x = x_ref[...]
    h0 = mm_t(d, jnp.concatenate([g_ref[0, 0], g_ref[0, 1]], axis=0), PICK)
    h0r = h0[:, :width]
    h0i = h0[:, width:]
    u_ri = mm(jnp.concatenate([x[:width], x[width:]], axis=1), jnp.concatenate(
        [jnp.concatenate([h0r, h0i], axis=1), jnp.concatenate([-h0i, h0r], axis=1)], axis=0
    ))
    g1_rows = []
    for p in range(2):
        g1_rows += [g_ref[1, p, pl.ds(start, size), :] for start, size in order]
    g1 = mm_t(jnp.concatenate(g1_rows, axis=0), c_t, PICK)
    cols = lax.broadcasted_iota(jnp.int32, (width, width), 1)
    taken = jnp.zeros((width, width), jnp.int32)
    at = 0
    for start, size in order:
        inside = (cols >= at) & (cols < at + size)
        taken = jnp.where(inside, cols - at + start, taken)
        at += size
    arrive = (rows == taken).astype(F32)
    g2 = jnp.dot(jnp.concatenate([h_ref[0, 0], h_ref[0, 1]], axis=0), arrive, precision=PICK, preferred_element_type=F32)
    m_ref[...] = mm(complex_block(h_ref[1, 0], h_ref[1, 1]), g2)
    y = mm(complex_block(g1[:width], g1[width:]), jnp.concatenate([u_ri[:, :width], u_ri[:, width:]], axis=0))
    y_ref[pl.ds(0, width, stride=2), :] = y[:width]
    y_ref[pl.ds(1, width, stride=2), :] = y[width:]


def second_kernel(w_ref, m_ref, z_ref):
    width = m_ref.shape[-1]
    w = jnp.concatenate([w_ref[pl.ds(0, width, stride=2), :], w_ref[pl.ds(1, width, stride=2), :]], axis=0)
    z = mm(complex_block(m_ref[:width], m_ref[width:]), w)
    z_ref[pl.ds(0, width, stride=2), :] = z[:width]
    z_ref[pl.ds(1, width, stride=2), :] = z[width:]


def send_order(width):
    n_node = lax.axis_size("node")
    n_dev = lax.axis_size("dev")
    size = width // (n_node * n_dev)
    return tuple(((m // n_dev + n_node * (m % n_dev)) * size, size) for m in range(n_node * n_dev))


def exchange(y, width):
    parts = lax.axis_size("dev") * lax.axis_size("node")
    if width % parts == 0:
        return lax.all_to_all(y, ("node", "dev"), 0, 0, tiled=True)
    axes = ("dev", "node")
    split = parts // width
    v = y.reshape(width, 2, split, width // split).transpose(0, 2, 1, 3)
    v = lax.all_to_all(v.reshape(parts, -1), axes, 0, 0, tiled=True)
    v = v.reshape(width, split, 2, width // split).transpose(0, 2, 1, 3)
    return v.reshape(width, 2, width)


def local(state, gates, qubit_order):
    gbits = gates.shape[-1].bit_length() - 1
    width = 2**gbits
    parts = lax.axis_size("dev") * lax.axis_size("node")
    if width % parts == 0:
        order = send_order(width)
    else:
        order = ((0, width),)
    rows = state.reshape(2, width, width).transpose(1, 0, 2).reshape(2 * width, width)
    vmem = pl.BlockSpec(memory_space=pltpu.VMEM)
    y, m = pl.pallas_call(
        lambda *refs: first_kernel(*refs, gbits=gbits, order=order),
        out_shape=(pltpu.VMEM((2 * width, width), F32), pltpu.VMEM((2 * width, width), F32)),
        grid=(1,),
        in_specs=[
            pl.BlockSpec(memory_space=pltpu.SMEM),
            pl.BlockSpec((2 * width, width), lambda i: (0, 0)),
            pl.BlockSpec((2, 2, width, width), lambda i: (0, 0, 0, 0)),
            pl.BlockSpec((2, 2, width, width), lambda i: (1, 0, 0, 0)),
        ],
        out_specs=(vmem, vmem),
        scratch_shapes=[pltpu.VMEM((2 * width, width), F32), pltpu.SMEM((2 * (gbits + 1),), jnp.int32)],
    )(qubit_order.astype(jnp.int32), rows, gates, gates)
    w = exchange(y.reshape(width, 2, width), width).reshape(2 * width, width)
    z = pl.pallas_call(
        second_kernel,
        out_shape=jax.ShapeDtypeStruct((2 * width, width), F32),
        in_specs=[vmem, vmem],
        out_specs=pl.BlockSpec(memory_space=pltpu.VMEM),
    )(pltpu.with_memory_space_constraint(w, pltpu.VMEM), pltpu.with_memory_space_constraint(m, pltpu.VMEM))
    return z.reshape(width, 2, width).transpose(1, 0, 2).reshape(2, -1)


def solution(mesh):
    return jax.shard_map(
        local,
        mesh=mesh,
        in_specs=(P(None, ("node", "dev")), P(), P()),
        out_specs=P(None, ("node", "dev")),
        check_vma=False,
    )
```

```python
import jax
import jax.numpy as jnp
from jax import lax
from jax.experimental import pallas as pl
from jax.experimental.pallas import tpu as pltpu
from jax.sharding import PartitionSpec as P

HI = lax.Precision.HIGHEST
F32 = jnp.float32


def mm(a, b):
    return jnp.dot(a, b, precision=HI, preferred_element_type=F32)


def mm_t(a, b, precision=HI):
    return lax.dot_general(a, b, (((1,), (1,)), ((), ())), precision=precision, preferred_element_type=F32)


PICK = lax.Precision.HIGH


def flip_bit(x, index, u, axis):
    n = x.shape[axis]
    step = 2**u
    one = pltpu.roll(x, step, axis)
    other = pltpu.roll(x, n - step, axis)
    moved = pltpu.roll(index, step, axis)
    return jnp.where(moved == (index ^ step), one, other)


def complex_block(gr, gi):
    return jnp.concatenate(
        [jnp.concatenate([gr, -gi], axis=1), jnp.concatenate([gi, gr], axis=1)], axis=0
    )


def first_kernel(q_ref, s_ref, g_ref, h_ref, y_ref, m_ref, x_ref, pair_ref, *, gbits, order):
    width = 2**gbits
    cols = lax.broadcasted_iota(jnp.int32, (width, width), 1)
    taken = jnp.zeros((width, width), jnp.int32)
    at = 0
    for start, size in order:
        inside = (cols >= at) & (cols < at + size)
        taken = jnp.where(inside, cols - at + start, taken)
        at += size
    arrive = (lax.broadcasted_iota(jnp.int32, (width, width), 0) == taken).astype(F32)
    g2 = jnp.dot(jnp.concatenate([h_ref[0, 0], h_ref[0, 1]], axis=0), arrive, precision=PICK, preferred_element_type=F32)
    m_ref[...] = mm(complex_block(h_ref[1, 0], h_ref[1, 1]), g2)
    q = [q_ref[j] for j in range(2 * gbits)]
    for slot in range(2 * (gbits + 1)):
        pair_ref[slot] = gbits
    rank_col = 0
    rank_row = 0
    for t in range(gbits):
        col_cross = q[t] >= gbits
        row_cross = q[gbits + t] < gbits
        pair_ref[jnp.where(col_cross, rank_col, gbits)] = q[t] - gbits
        pair_ref[gbits + 1 + jnp.where(row_cross, rank_row, gbits)] = q[gbits + t]
        rank_col = rank_col + jnp.where(col_cross, 1, 0)
        rank_row = rank_row + jnp.where(row_cross, 1, 0)
    row_of = [pair_ref[i] for i in range(gbits)]
    col_of = [pair_ref[gbits + 1 + i] for i in range(gbits)]
    partner = [gbits] * gbits
    partner_back = [gbits] * gbits
    for i in range(gbits):
        for a in range(gbits):
            partner[a] = jnp.where(row_of[i] == a, col_of[i], partner[a])
            partner_back[a] = jnp.where(col_of[i] == a, row_of[i], partner_back[a])
    row_cross = [partner[u] < gbits for u in range(gbits)]
    col_cross = [partner_back[u] < gbits for u in range(gbits)]
    held_at = 0
    for u in range(gbits):
        pair_ref[jnp.where(row_cross[u], gbits, held_at)] = u
        held_at = held_at + jnp.where(row_cross[u], 0, 1)
    kept = [pair_ref[u] for u in range(gbits)]
    col_pos = []
    stay_rank = 0
    for u in range(gbits):
        free = kept[0]
        for r in range(1, gbits):
            free = jnp.where(stay_rank == r, kept[r], free)
        col_pos.append(jnp.where(col_cross[u], partner_back[u], free))
        stay_rank = stay_rank + jnp.where(col_cross[u], 0, 1)
    pos = []
    for j in range(2 * gbits):
        if j < gbits:
            src_col = col_pos[0]
            for u in range(1, gbits):
                src_col = jnp.where(q[j] == u, col_pos[u], src_col)
            pos.append(jnp.where(q[j] >= gbits, q[j] - gbits, src_col))
        else:
            back = partner_back[0]
            for u in range(1, gbits):
                back = jnp.where(q[j] == u, partner_back[u], back)
            pos.append(jnp.where(q[j] < gbits, back, q[j] - gbits))
    lane = lax.broadcasted_iota(jnp.int32, (1, width), 1)
    col_to = jnp.zeros((1, width), jnp.int32)
    row_from = jnp.zeros((1, width), jnp.int32)
    col_from = jnp.zeros((1, width), jnp.int32)
    for t in range(gbits):
        col_to = col_to + jnp.left_shift(jnp.right_shift(lane, t) & 1, col_pos[t])
        row_from = row_from + jnp.left_shift(jnp.right_shift(lane, t) & 1, pos[gbits + t])
        col_from = col_from + jnp.left_shift(jnp.right_shift(lane, t) & 1, pos[t])
    rows = lax.broadcasted_iota(jnp.int32, (width, width), 0)
    b_t = (rows == col_to).astype(F32)
    c_t = (rows == row_from).astype(F32)
    d = (rows == col_from).astype(F32)
    x = jnp.concatenate(
        [s_ref[pl.ds(0, width, stride=2), :], s_ref[pl.ds(1, width, stride=2), :]], axis=0
    )
    x = mm_t(x, b_t, PICK)
    rows2 = lax.broadcasted_iota(jnp.int32, (2 * width, width), 0)
    cols2 = lax.broadcasted_iota(jnp.int32, (2 * width, width), 1)
    for u in range(gbits):
        flipped = flip_bit(flip_bit(x, rows2, u, 0), cols2, u, 1)
        differ = (jnp.right_shift(rows2 ^ cols2, u) & 1) == 1
        x = jnp.where(differ & row_cross[u], flipped, x)
    x_ref[...] = x
    x = x_ref[...]
    h0 = mm_t(d, jnp.concatenate([g_ref[0, 0], g_ref[0, 1]], axis=0), PICK)
    h0r = h0[:, :width]
    h0i = h0[:, width:]
    u_ri = mm(jnp.concatenate([x[:width], x[width:]], axis=1), jnp.concatenate(
        [jnp.concatenate([h0r, h0i], axis=1), jnp.concatenate([-h0i, h0r], axis=1)], axis=0
    ))
    g1_rows = []
    for p in range(2):
        g1_rows += [g_ref[1, p, pl.ds(start, size), :] for start, size in order]
    g1 = mm_t(jnp.concatenate(g1_rows, axis=0), c_t, PICK)
    y = mm(complex_block(g1[:width], g1[width:]), jnp.concatenate([u_ri[:, :width], u_ri[:, width:]], axis=0))
    y_ref[pl.ds(0, width, stride=2), :] = y[:width]
    y_ref[pl.ds(1, width, stride=2), :] = y[width:]


def second_kernel(w_ref, m_ref, z_ref):
    width = m_ref.shape[-1]
    w = jnp.concatenate([w_ref[pl.ds(0, width, stride=2), :], w_ref[pl.ds(1, width, stride=2), :]], axis=0)
    z = mm(complex_block(m_ref[:width], m_ref[width:]), w)
    z_ref[pl.ds(0, width, stride=2), :] = z[:width]
    z_ref[pl.ds(1, width, stride=2), :] = z[width:]


def send_order(width):
    n_node = lax.axis_size("node")
    n_dev = lax.axis_size("dev")
    size = width // (n_node * n_dev)
    return tuple(((m // n_dev + n_node * (m % n_dev)) * size, size) for m in range(n_node * n_dev))


def exchange(y, width):
    parts = lax.axis_size("dev") * lax.axis_size("node")
    if width % parts == 0:
        return lax.all_to_all(y, ("node", "dev"), 0, 0, tiled=True)
    axes = ("dev", "node")
    split = parts // width
    v = y.reshape(width, 2, split, width // split).transpose(0, 2, 1, 3)
    v = lax.all_to_all(v.reshape(parts, -1), axes, 0, 0, tiled=True)
    v = v.reshape(width, split, 2, width // split).transpose(0, 2, 1, 3)
    return v.reshape(width, 2, width)


def local(state, gates, qubit_order):
    gbits = gates.shape[-1].bit_length() - 1
    width = 2**gbits
    parts = lax.axis_size("dev") * lax.axis_size("node")
    if width % parts == 0:
        order = send_order(width)
    else:
        order = ((0, width),)
    rows = state.reshape(2, width, width).transpose(1, 0, 2).reshape(2 * width, width)
    vmem = pl.BlockSpec(memory_space=pltpu.VMEM)
    y, m = pl.pallas_call(
        lambda *refs: first_kernel(*refs, gbits=gbits, order=order),
        out_shape=(pltpu.VMEM((2 * width, width), F32), pltpu.VMEM((2 * width, width), F32)),
        grid=(1,),
        in_specs=[
            pl.BlockSpec(memory_space=pltpu.SMEM),
            pl.BlockSpec((2 * width, width), lambda i: (0, 0)),
            pl.BlockSpec((2, 2, width, width), lambda i: (0, 0, 0, 0)),
            pl.BlockSpec((2, 2, width, width), lambda i: (1, 0, 0, 0)),
        ],
        out_specs=(vmem, vmem),
        scratch_shapes=[pltpu.VMEM((2 * width, width), F32), pltpu.SMEM((2 * (gbits + 1),), jnp.int32)],
    )(qubit_order.astype(jnp.int32), rows, gates, gates)
    w = exchange(y.reshape(width, 2, width), width).reshape(2 * width, width)
    z = pl.pallas_call(
        second_kernel,
        out_shape=jax.ShapeDtypeStruct((2 * width, width), F32),
        in_specs=[vmem, vmem],
        out_specs=pl.BlockSpec(memory_space=pltpu.VMEM),
    )(pltpu.with_memory_space_constraint(w, pltpu.VMEM), pltpu.with_memory_space_constraint(m, pltpu.VMEM))
    return z.reshape(width, 2, width).transpose(1, 0, 2).reshape(2, -1)


def solution(mesh):
    return jax.shard_map(
        local,
        mesh=mesh,
        in_specs=(P(None, ("node", "dev")), P(), P()),
        out_specs=P(None, ("node", "dev")),
        check_vma=False,
    )
```

```python
import jax
import jax.numpy as jnp
from jax import lax
from jax.experimental import pallas as pl
from jax.experimental.pallas import tpu as pltpu
from jax.sharding import PartitionSpec as P

HI = lax.Precision.HIGHEST
F32 = jnp.float32


def mm(a, b):
    return jnp.dot(a, b, precision=HI, preferred_element_type=F32)


def mm_t(a, b, precision=HI):
    return lax.dot_general(a, b, (((1,), (1,)), ((), ())), precision=precision, preferred_element_type=F32)


PICK = lax.Precision.HIGH


def flip_bit(x, index, u, axis):
    n = x.shape[axis]
    step = 2**u
    one = pltpu.roll(x, step, axis)
    other = pltpu.roll(x, n - step, axis)
    moved = pltpu.roll(index, step, axis)
    return jnp.where(moved == (index ^ step), one, other)


def complex_block(gr, gi):
    return jnp.concatenate(
        [jnp.concatenate([gr, -gi], axis=1), jnp.concatenate([gi, gr], axis=1)], axis=0
    )


def first_kernel(q_ref, s_ref, g_ref, h_ref, y_ref, m_ref, x_ref, pair_ref, *, gbits, order):
    width = 2**gbits
    cols = lax.broadcasted_iota(jnp.int32, (width, width), 1)
    taken = jnp.zeros((width, width), jnp.int32)
    at = 0
    for start, size in order:
        inside = (cols >= at) & (cols < at + size)
        taken = jnp.where(inside, cols - at + start, taken)
        at += size
    arrive = (lax.broadcasted_iota(jnp.int32, (width, width), 0) == taken).astype(F32)
    g2 = jnp.dot(jnp.concatenate([h_ref[0, 0], h_ref[0, 1]], axis=0), arrive, precision=PICK, preferred_element_type=F32)
    m_ref[...] = mm(complex_block(h_ref[1, 0], h_ref[1, 1]), g2)
    q = [q_ref[j] for j in range(2 * gbits)]
    for slot in range(2 * (gbits + 1)):
        pair_ref[slot] = gbits
    rank_col = 0
    rank_row = 0
    for t in range(gbits):
        col_cross = q[t] >= gbits
        row_cross = q[gbits + t] < gbits
        pair_ref[jnp.where(col_cross, rank_col, gbits)] = q[t] - gbits
        pair_ref[gbits + 1 + jnp.where(row_cross, rank_row, gbits)] = q[gbits + t]
        rank_col = rank_col + jnp.where(col_cross, 1, 0)
        rank_row = rank_row + jnp.where(row_cross, 1, 0)
    row_of = [pair_ref[i] for i in range(gbits)]
    col_of = [pair_ref[gbits + 1 + i] for i in range(gbits)]
    pt, bk, kp, cp = 2 * (gbits + 1), 3 * (gbits + 1), 4 * (gbits + 1), 5 * (gbits + 1)
    for u in range(gbits):
        pair_ref[pt + u] = gbits
        pair_ref[bk + u] = gbits
    for i in range(gbits):
        pair_ref[pt + row_of[i]] = col_of[i]
        pair_ref[bk + col_of[i]] = row_of[i]
    partner = [pair_ref[pt + u] for u in range(gbits)]
    partner_back = [pair_ref[bk + u] for u in range(gbits)]
    row_cross = [partner[u] < gbits for u in range(gbits)]
    col_cross = [partner_back[u] < gbits for u in range(gbits)]
    held_at = 0
    for u in range(gbits):
        pair_ref[kp + jnp.where(row_cross[u], gbits, held_at)] = u
        held_at = held_at + jnp.where(row_cross[u], 0, 1)
    col_pos = []
    stay_rank = 0
    for u in range(gbits):
        free = pair_ref[kp + jnp.minimum(stay_rank, gbits)]
        col_pos.append(jnp.where(col_cross[u], partner_back[u], free))
        pair_ref[cp + u] = col_pos[u]
        stay_rank = stay_rank + jnp.where(col_cross[u], 0, 1)
    pos = []
    for j in range(2 * gbits):
        low = jnp.where(q[j] < gbits, q[j], 0)
        if j < gbits:
            pos.append(jnp.where(q[j] >= gbits, q[j] - gbits, pair_ref[cp + low]))
        else:
            pos.append(jnp.where(q[j] < gbits, pair_ref[bk + low], q[j] - gbits))
    lane = lax.broadcasted_iota(jnp.int32, (1, width), 1)
    col_to = jnp.zeros((1, width), jnp.int32)
    row_from = jnp.zeros((1, width), jnp.int32)
    col_from = jnp.zeros((1, width), jnp.int32)
    for t in range(gbits):
        col_to = col_to + jnp.left_shift(jnp.right_shift(lane, t) & 1, col_pos[t])
        row_from = row_from + jnp.left_shift(jnp.right_shift(lane, t) & 1, pos[gbits + t])
        col_from = col_from + jnp.left_shift(jnp.right_shift(lane, t) & 1, pos[t])
    rows = lax.broadcasted_iota(jnp.int32, (width, width), 0)
    b_t = (rows == col_to).astype(F32)
    c_t = (rows == row_from).astype(F32)
    d = (rows == col_from).astype(F32)
    x = jnp.concatenate(
        [s_ref[pl.ds(0, width, stride=2), :], s_ref[pl.ds(1, width, stride=2), :]], axis=0
    )
    x = mm_t(x, b_t, PICK)
    rows2 = lax.broadcasted_iota(jnp.int32, (2 * width, width), 0)
    cols2 = lax.broadcasted_iota(jnp.int32, (2 * width, width), 1)
    for u in range(gbits):
        flipped = flip_bit(flip_bit(x, rows2, u, 0), cols2, u, 1)
        differ = (jnp.right_shift(rows2 ^ cols2, u) & 1) == 1
        x = jnp.where(differ & row_cross[u], flipped, x)
    x_ref[...] = x
    x = x_ref[...]
    h0 = mm_t(d, jnp.concatenate([g_ref[0, 0], g_ref[0, 1]], axis=0), PICK)
    h0r = h0[:, :width]
    h0i = h0[:, width:]
    u_ri = mm(jnp.concatenate([x[:width], x[width:]], axis=1), jnp.concatenate(
        [jnp.concatenate([h0r, h0i], axis=1), jnp.concatenate([-h0i, h0r], axis=1)], axis=0
    ))
    g1_rows = []
    for p in range(2):
        g1_rows += [g_ref[1, p, pl.ds(start, size), :] for start, size in order]
    g1 = mm_t(jnp.concatenate(g1_rows, axis=0), c_t, PICK)
    y = mm(complex_block(g1[:width], g1[width:]), jnp.concatenate([u_ri[:, :width], u_ri[:, width:]], axis=0))
    y_ref[pl.ds(0, width, stride=2), :] = y[:width]
    y_ref[pl.ds(1, width, stride=2), :] = y[width:]


def second_kernel(w_ref, m_ref, z_ref):
    width = m_ref.shape[-1]
    w = jnp.concatenate([w_ref[pl.ds(0, width, stride=2), :], w_ref[pl.ds(1, width, stride=2), :]], axis=0)
    z = mm(complex_block(m_ref[:width], m_ref[width:]), w)
    z_ref[pl.ds(0, width, stride=2), :] = z[:width]
    z_ref[pl.ds(1, width, stride=2), :] = z[width:]


def send_order(width):
    n_node = lax.axis_size("node")
    n_dev = lax.axis_size("dev")
    size = width // (n_node * n_dev)
    return tuple(((m // n_dev + n_node * (m % n_dev)) * size, size) for m in range(n_node * n_dev))


def exchange(y, width):
    parts = lax.axis_size("dev") * lax.axis_size("node")
    if width % parts == 0:
        return lax.all_to_all(y, ("node", "dev"), 0, 0, tiled=True)
    axes = ("dev", "node")
    split = parts // width
    v = y.reshape(width, 2, split, width // split).transpose(0, 2, 1, 3)
    v = lax.all_to_all(v.reshape(parts, -1), axes, 0, 0, tiled=True)
    v = v.reshape(width, split, 2, width // split).transpose(0, 2, 1, 3)
    return v.reshape(width, 2, width)


def local(state, gates, qubit_order):
    gbits = gates.shape[-1].bit_length() - 1
    width = 2**gbits
    parts = lax.axis_size("dev") * lax.axis_size("node")
    if width % parts == 0:
        order = send_order(width)
    else:
        order = ((0, width),)
    rows = state.reshape(2, width, width).transpose(1, 0, 2).reshape(2 * width, width)
    vmem = pl.BlockSpec(memory_space=pltpu.VMEM)
    y, m = pl.pallas_call(
        lambda *refs: first_kernel(*refs, gbits=gbits, order=order),
        out_shape=(pltpu.VMEM((2 * width, width), F32), pltpu.VMEM((2 * width, width), F32)),
        grid=(1,),
        in_specs=[
            pl.BlockSpec(memory_space=pltpu.SMEM),
            pl.BlockSpec((2 * width, width), lambda i: (0, 0)),
            pl.BlockSpec((2, 2, width, width), lambda i: (0, 0, 0, 0)),
            pl.BlockSpec((2, 2, width, width), lambda i: (1, 0, 0, 0)),
        ],
        out_specs=(vmem, vmem),
        scratch_shapes=[pltpu.VMEM((2 * width, width), F32), pltpu.SMEM((6 * (gbits + 1),), jnp.int32)],
    )(qubit_order.astype(jnp.int32), rows, gates, gates)
    w = exchange(y.reshape(width, 2, width), width).reshape(2 * width, width)
    z = pl.pallas_call(
        second_kernel,
        out_shape=jax.ShapeDtypeStruct((2 * width, width), F32),
        in_specs=[vmem, vmem],
        out_specs=pl.BlockSpec(memory_space=pltpu.VMEM),
    )(pltpu.with_memory_space_constraint(w, pltpu.VMEM), pltpu.with_memory_space_constraint(m, pltpu.VMEM))
    return z.reshape(width, 2, width).transpose(1, 0, 2).reshape(2, -1)


def solution(mesh):
    return jax.shard_map(
        local,
        mesh=mesh,
        in_specs=(P(None, ("node", "dev")), P(), P()),
        out_specs=P(None, ("node", "dev")),
        check_vma=False,
    )
```

```python
import jax
import jax.numpy as jnp
from jax import lax
from jax.experimental import pallas as pl
from jax.experimental.pallas import tpu as pltpu
from jax.sharding import PartitionSpec as P

HI = lax.Precision.HIGHEST
F32 = jnp.float32


def mm(a, b):
    return jnp.dot(a, b, precision=HI, preferred_element_type=F32)


def mm_t(a, b, precision=HI):
    return lax.dot_general(a, b, (((1,), (1,)), ((), ())), precision=precision, preferred_element_type=F32)


PICK = lax.Precision.HIGH


def flip_bit(x, index, u, axis):
    n = x.shape[axis]
    step = 2**u
    one = pltpu.roll(x, step, axis)
    other = pltpu.roll(x, n - step, axis)
    moved = pltpu.roll(index, step, axis)
    return jnp.where(moved == (index ^ step), one, other)


def complex_block(gr, gi):
    return jnp.concatenate(
        [jnp.concatenate([gr, -gi], axis=1), jnp.concatenate([gi, gr], axis=1)], axis=0
    )


def first_kernel(q_ref, s_ref, g_ref, h_ref, y_ref, m_ref, x_ref, pair_ref, *, gbits, order):
    width = 2**gbits
    cols = lax.broadcasted_iota(jnp.int32, (width, width), 1)
    taken = jnp.zeros((width, width), jnp.int32)
    at = 0
    for start, size in order:
        inside = (cols >= at) & (cols < at + size)
        taken = jnp.where(inside, cols - at + start, taken)
        at += size
    arrive = (lax.broadcasted_iota(jnp.int32, (width, width), 0) == taken).astype(F32)
    g2 = jnp.dot(jnp.concatenate([h_ref[0, 0], h_ref[0, 1]], axis=0), arrive, precision=PICK, preferred_element_type=F32)
    m_ref[...] = mm(complex_block(h_ref[1, 0], h_ref[1, 1]), g2)
    q = [q_ref[j] for j in range(2 * gbits)]
    for slot in range(2 * (gbits + 1)):
        pair_ref[slot] = gbits
    rank_col = 0
    rank_row = 0
    for t in range(gbits):
        col_cross = q[t] >= gbits
        row_cross = q[gbits + t] < gbits
        pair_ref[jnp.where(col_cross, rank_col, gbits)] = q[t] - gbits
        pair_ref[gbits + 1 + jnp.where(row_cross, rank_row, gbits)] = q[gbits + t]
        rank_col = rank_col + jnp.where(col_cross, 1, 0)
        rank_row = rank_row + jnp.where(row_cross, 1, 0)
    row_of = [pair_ref[i] for i in range(gbits)]
    col_of = [pair_ref[gbits + 1 + i] for i in range(gbits)]
    pt, bk, kp, cp = 2 * (gbits + 1), 3 * (gbits + 1), 4 * (gbits + 1), 5 * (gbits + 1)
    for u in range(gbits):
        pair_ref[pt + u] = gbits
        pair_ref[bk + u] = gbits
    for i in range(gbits):
        pair_ref[pt + row_of[i]] = col_of[i]
        pair_ref[bk + col_of[i]] = row_of[i]
    partner = [pair_ref[pt + u] for u in range(gbits)]
    partner_back = [pair_ref[bk + u] for u in range(gbits)]
    row_cross = [partner[u] < gbits for u in range(gbits)]
    col_cross = [partner_back[u] < gbits for u in range(gbits)]
    held_at = 0
    for u in range(gbits):
        pair_ref[kp + jnp.where(row_cross[u], gbits, held_at)] = u
        held_at = held_at + jnp.where(row_cross[u], 0, 1)
    col_pos = []
    stay_rank = 0
    for u in range(gbits):
        free = pair_ref[kp + jnp.minimum(stay_rank, gbits)]
        col_pos.append(jnp.where(col_cross[u], partner_back[u], free))
        pair_ref[cp + u] = col_pos[u]
        stay_rank = stay_rank + jnp.where(col_cross[u], 0, 1)
    pos = []
    for j in range(2 * gbits):
        low = jnp.where(q[j] < gbits, q[j], 0)
        if j < gbits:
            pos.append(jnp.where(q[j] >= gbits, q[j] - gbits, pair_ref[cp + low]))
        else:
            pos.append(jnp.where(q[j] < gbits, pair_ref[bk + low], q[j] - gbits))
    lane = lax.broadcasted_iota(jnp.int32, (1, width), 1)
    col_to = jnp.zeros((1, width), jnp.int32)
    row_from = jnp.zeros((1, width), jnp.int32)
    col_from = jnp.zeros((1, width), jnp.int32)
    for t in range(gbits):
        col_to = col_to + jnp.left_shift(jnp.right_shift(lane, t) & 1, col_pos[t])
        row_from = row_from + jnp.left_shift(jnp.right_shift(lane, t) & 1, pos[gbits + t])
        col_from = col_from + jnp.left_shift(jnp.right_shift(lane, t) & 1, pos[t])
    rows = lax.broadcasted_iota(jnp.int32, (width, width), 0)
    b_t = (rows == col_to).astype(F32)
    c_t = (rows == row_from).astype(F32)
    d = (rows == col_from).astype(F32)
    x = jnp.concatenate(
        [s_ref[pl.ds(0, width, stride=2), :], s_ref[pl.ds(1, width, stride=2), :]], axis=0
    )
    x = mm_t(x, b_t, PICK)
    rows2 = lax.broadcasted_iota(jnp.int32, (2 * width, width), 0)
    cols2 = lax.broadcasted_iota(jnp.int32, (2 * width, width), 1)
    for u in range(gbits):
        flipped = flip_bit(flip_bit(x, rows2, u, 0), cols2, u, 1)
        differ = (jnp.right_shift(rows2 ^ cols2, u) & 1) == 1
        x = jnp.where(differ & row_cross[u], flipped, x)
    h0 = mm_t(d, jnp.concatenate([g_ref[0, 0], g_ref[0, 1]], axis=0), PICK)
    h0r = h0[:, :width]
    h0i = h0[:, width:]
    u_ri = mm(jnp.concatenate([x[:width], x[width:]], axis=1), jnp.concatenate(
        [jnp.concatenate([h0r, h0i], axis=1), jnp.concatenate([-h0i, h0r], axis=1)], axis=0
    ))
    g1_rows = []
    for p in range(2):
        g1_rows += [g_ref[1, p, pl.ds(start, size), :] for start, size in order]
    g1 = mm_t(jnp.concatenate(g1_rows, axis=0), c_t, PICK)
    y = mm(complex_block(g1[:width], g1[width:]), jnp.concatenate([u_ri[:, :width], u_ri[:, width:]], axis=0))
    y_ref[pl.ds(0, width, stride=2), :] = y[:width]
    y_ref[pl.ds(1, width, stride=2), :] = y[width:]


def second_kernel(w_ref, m_ref, z_ref):
    width = m_ref.shape[-1]
    w = jnp.concatenate([w_ref[pl.ds(0, width, stride=2), :], w_ref[pl.ds(1, width, stride=2), :]], axis=0)
    z = mm(complex_block(m_ref[:width], m_ref[width:]), w)
    z_ref[pl.ds(0, width, stride=2), :] = z[:width]
    z_ref[pl.ds(1, width, stride=2), :] = z[width:]


def send_order(width):
    n_node = lax.axis_size("node")
    n_dev = lax.axis_size("dev")
    size = width // (n_node * n_dev)
    return tuple(((m // n_dev + n_node * (m % n_dev)) * size, size) for m in range(n_node * n_dev))


def exchange(y, width):
    parts = lax.axis_size("dev") * lax.axis_size("node")
    if width % parts == 0:
        return lax.all_to_all(y, ("node", "dev"), 0, 0, tiled=True)
    axes = ("dev", "node")
    split = parts // width
    v = y.reshape(width, 2, split, width // split).transpose(0, 2, 1, 3)
    v = lax.all_to_all(v.reshape(parts, -1), axes, 0, 0, tiled=True)
    v = v.reshape(width, split, 2, width // split).transpose(0, 2, 1, 3)
    return v.reshape(width, 2, width)


def local(state, gates, qubit_order):
    gbits = gates.shape[-1].bit_length() - 1
    width = 2**gbits
    parts = lax.axis_size("dev") * lax.axis_size("node")
    if width % parts == 0:
        order = send_order(width)
    else:
        order = ((0, width),)
    rows = state.reshape(2, width, width).transpose(1, 0, 2).reshape(2 * width, width)
    vmem = pl.BlockSpec(memory_space=pltpu.VMEM)
    y, m = pl.pallas_call(
        lambda *refs: first_kernel(*refs, gbits=gbits, order=order),
        out_shape=(pltpu.VMEM((2 * width, width), F32), pltpu.VMEM((2 * width, width), F32)),
        grid=(1,),
        in_specs=[
            pl.BlockSpec(memory_space=pltpu.SMEM),
            pl.BlockSpec((2 * width, width), lambda i: (0, 0)),
            pl.BlockSpec((2, 2, width, width), lambda i: (0, 0, 0, 0)),
            pl.BlockSpec((2, 2, width, width), lambda i: (1, 0, 0, 0)),
        ],
        out_specs=(vmem, vmem),
        scratch_shapes=[pltpu.VMEM((2 * width, width), F32), pltpu.SMEM((6 * (gbits + 1),), jnp.int32)],
    )(qubit_order.astype(jnp.int32), rows, gates, gates)
    w = exchange(y.reshape(width, 2, width), width).reshape(2 * width, width)
    z = pl.pallas_call(
        second_kernel,
        out_shape=jax.ShapeDtypeStruct((2 * width, width), F32),
        in_specs=[vmem, vmem],
        out_specs=pl.BlockSpec(memory_space=pltpu.VMEM),
    )(pltpu.with_memory_space_constraint(w, pltpu.VMEM), pltpu.with_memory_space_constraint(m, pltpu.VMEM))
    return z.reshape(width, 2, width).transpose(1, 0, 2).reshape(2, -1)


def solution(mesh):
    return jax.shard_map(
        local,
        mesh=mesh,
        in_specs=(P(None, ("node", "dev")), P(), P()),
        out_specs=P(None, ("node", "dev")),
        check_vma=False,
    )
```
